128 devices in a mesh: sky: 4 (over y), visit: 32 (over x, z, core).
Axes of the slice: x: 4, y: 4, z: 4, core: 2. Of those that a mesh axis runs over, the one named last changes fastest.
Arguments:
- sky_image: float32 [6, 2048, 16384], P(None, 'sky', 'visit'), may hold values from -6 to 6
- observed: bfloat16 [768, 512, 512], P(('sky', 'visit')), may hold values from -6 to 6
- footprint: int32 [768, 2], P(('sky', 'visit')), may hold values from 0 to 123, as said below
- segment_band: int32 [768], P(('sky', 'visit')), may hold values from 0 to 5
- offsets: int32 [768, 2], P(('sky', 'visit')), may hold values from 0 to 127
- psf_rows: bfloat16 [4, 512, 512], replicated, may hold values from -0.25 to 0.25
- psf_cols: bfloat16 [4, 512, 512], replicated, may hold values from -0.25 to 0.25
- psf_weights: float32 [768, 4], P(('sky', 'visit')), may hold values from 0.2 to 1
- step_sizes: float32 [6], replicated, may hold values from 0.05 to 0.5
Outputs:
- updated_sky: float32 [6, 2048, 16384], P(None, 'sky', 'visit')
The draws below stay inside these ranges and needn't reach their ends.
Inputs may be any that keep to these rules, and one draw needn't show every extreme that they name: Segment s is held by device s // 6 (row-major over sky then visit, owning the sky block of that position). Its footprint lies inside the sky and within 2 tiles of that device's block on every side; on every device whose block does not touch the sky's border, some segment's footprint starts 2 tiles before the block in rows and columns and some segment's footprint ends 2 tiles after it.
All inputs are finite; a program needn't handle non-finite values.
Results may differ from the reference program's by a relative error of at most 0.0095.
Values may be sent and summed in bfloat16 or wider, within the bound.
No kernel may reach another device: no remote copies, remote signals or barrier semaphores. Data moves between devices by JAX's collectives and lax.ppermute only.
A program may use at most 192 MiB of HBM per device.

```python
import math
import jax
import jax.numpy as jnp
from jax import lax

BANDS = 6
TILE = 128
PIX = 512
PSF_TERMS = 4
SEG_DEV = 6
SIDE = 4
SPAN = 5
ROWS_PX = 2048
COLS_PX = 16384
GRID_ROWS = 16
GRID_COLS = 128
SEGMENTS = 768
DEVICES = 128


def shuffle_roles(role_key):
    return jax.random.permutation(role_key, SEG_DEV).astype(jnp.int32)


def draw_footprint(key, part):
    seg_ids = jnp.arange(SEGMENTS, dtype=jnp.int32)
    device_ids = seg_ids // SEG_DEV
    blocks_across = GRID_COLS // SIDE
    block_row = device_ids // blocks_across
    block_col = device_ids % blocks_across
    local_pos = jax.random.randint(jax.random.fold_in(key, 3), (SEGMENTS, 2), 0, SIDE).astype(jnp.int32)
    role_keys = jax.random.split(jax.random.fold_in(key, 5), DEVICES)
    roles = jax.vmap(shuffle_roles)(role_keys).reshape(SEGMENTS)
    local_pos = jnp.where((roles == 0)[:, None], 0, jnp.where((roles == 1)[:, None], SIDE - 1, local_pos)).astype(jnp.int32)
    half_span = SPAN // 2
    first_row = jnp.clip(block_row * SIDE + local_pos[:, 0] - half_span, 0, GRID_ROWS - SPAN)
    first_col = jnp.clip(block_col * SIDE + local_pos[:, 1] - half_span, 0, GRID_COLS - SPAN)
    return jnp.stack([first_row, first_col], axis=1).astype(jnp.int32)


def plant(array, key, low, largest):
    spot = [jax.random.randint(jax.random.fold_in(key, axis), (), 0, length) for axis, length in enumerate(array.shape)]
    main_axis = array.shape.index(max(array.shape))
    next_to = spot[:main_axis] + [(spot[main_axis] + 1) % array.shape[main_axis]] + spot[main_axis + 1:]
    return array.at[tuple(spot)].set(low).at[tuple(next_to)].set(largest)


def level_of(stream_key, extent, cuts, least, largest):
    def one(axis_at, blocks):
        draws = jax.random.uniform(jax.random.fold_in(jax.random.fold_in(stream_key, 6), axis_at), (blocks,), jnp.float32, least / len(cuts), largest / len(cuts))
        return jnp.repeat(jnp.exp(draws), extent[axis_at] // blocks).reshape((-1,) + (1,) * (len(extent) - axis_at - 1))

    loudness = one(*cuts[0])
    for cut in cuts[1:]:
        loudness = loudness * one(*cut)
    return loudness


def scatter_about(own_key, dims, deviation, limit, cuts=(), held_as=jnp.bfloat16):
    values = deviation * jax.random.normal(own_key, dims, jnp.float32)
    if cuts:
        values = values * level_of(own_key, dims, cuts, -0.22, 0.18)
    return jnp.clip(values, -limit, limit).astype(held_as)


def setup_inputs(seed: int = 0) -> dict:
    arg_keys = jax.random.split(jax.random.key(seed), 10)
    return {
        "sky_image": scatter_about(arg_keys[0], (BANDS, ROWS_PX, COLS_PX), 1.0, 6.0, ((1, 4), (2, 32)), jnp.float32),
        "observed": scatter_about(arg_keys[1], (SEGMENTS, PIX, PIX), 1.0, 6.0, ((0, 128),)),
        "footprint": draw_footprint(jax.random.fold_in(arg_keys[9], 71), 0),
        "segment_band": plant(jax.random.randint(arg_keys[3], (SEGMENTS,), 0, BANDS), jax.random.fold_in(arg_keys[3], 1), 0, BANDS - 1).astype(jnp.int32),
        "offsets": plant(jax.random.randint(arg_keys[4], (SEGMENTS, 2), 0, TILE), jax.random.fold_in(arg_keys[4], 1), 0, TILE - 1).astype(jnp.int32),
        "psf_rows": scatter_about(arg_keys[5], (PSF_TERMS, PIX, PIX), PIX ** -0.5, 0.25),
        "psf_cols": scatter_about(arg_keys[6], (PSF_TERMS, PIX, PIX), PIX ** -0.5, 0.25),
        "psf_weights": jnp.clip(jnp.exp(math.log(1.0) - 1.609438 * jax.random.uniform(arg_keys[7], (SEGMENTS, PSF_TERMS), jnp.float32) ** level_of(arg_keys[7], (SEGMENTS, PSF_TERMS), ((0, 128),), -0.2, 0.2)), 0.2, 1.0),
        "step_sizes": jnp.clip(jnp.exp(jax.random.uniform(arg_keys[8], (BANDS,), jnp.float32, math.log(0.05), math.log(0.5))), 0.05, 0.5),
    }


def reference(sky_image, observed, footprint, segment_band, offsets, psf_rows, psf_cols, psf_weights, step_sizes):
    sky_bf = sky_image.astype(jnp.bfloat16)
    rows_wide = psf_rows.astype(jnp.float32)
    cols_wide = psf_cols.astype(jnp.float32)
    rows_flat = psf_rows.reshape(PSF_TERMS * PIX, PIX)
    top_rows = (footprint[:, 0] * TILE + offsets[:, 0]).astype(jnp.int32)
    left_cols = (footprint[:, 1] * TILE + offsets[:, 1]).astype(jnp.int32)
    band_ids = segment_band.astype(jnp.int32)

    def accumulate(gradient, packed):
        target, weights, band_index, top, left_col = packed
        window = lax.dynamic_slice(sky_bf, (band_index, top, left_col), (1, PIX, PIX))[0]
        left_terms = jnp.dot(rows_flat, window, preferred_element_type=jnp.float32).astype(jnp.bfloat16).reshape(PSF_TERMS, PIX, PIX)
        blurred = jnp.einsum("kij,klj->kil", left_terms.astype(jnp.float32), cols_wide)
        model_image = jnp.sum(weights[:, None, None] * blurred, axis=0)
        residual = (model_image - target.astype(jnp.float32)).astype(jnp.bfloat16)
        right_terms = jnp.einsum("ij,kjl->kil", residual.astype(jnp.float32), cols_wide).astype(jnp.bfloat16)
        spread = jnp.einsum("kji,kjl->kil", rows_wide, right_terms.astype(jnp.float32))
        adjoint = jnp.sum(weights[:, None, None] * spread, axis=0).astype(jnp.bfloat16)
        current = lax.dynamic_slice(gradient, (band_index, top, left_col), (1, PIX, PIX))
        gradient = lax.dynamic_update_slice(gradient, current + adjoint.astype(jnp.float32)[None], (band_index, top, left_col))
        return gradient, None

    empty_sum = jnp.zeros((BANDS, ROWS_PX, COLS_PX), jnp.float32)
    gradient, unused = lax.scan(accumulate, empty_sum, (observed, psf_weights, band_ids, top_rows, left_cols))
    return sky_image - step_sizes[:, None, None] * gradient
```

```python
import functools

import jax
import jax.numpy as jnp
from jax import lax
from jax.experimental import pallas as pl
from jax.experimental.pallas import tpu as pltpu
from jax.sharding import PartitionSpec as P

TILE = 128


def shift(value, axis, by):
    count = lax.axis_size(axis)
    pairs = [(i, i + by) for i in range(count) if 0 <= i + by < count]
    return lax.ppermute(value, axis, pairs)


def halo(block, rim):
    side = block.shape[1]
    up = shift(block[:, side - rim :, :], "sky", 1)
    down = shift(block[:, :rim, :], "sky", -1)
    left = shift(block[:, :, side - rim :], "visit", 1)
    right = shift(block[:, :, :rim], "visit", -1)
    from_left = shift(
        jnp.concatenate([up[:, :, side - rim :], down[:, :, side - rim :]], axis=1), "visit", 1
    )
    from_right = shift(jnp.concatenate([up[:, :, :rim], down[:, :, :rim]], axis=1), "visit", -1)
    top = jnp.concatenate([from_left[:, :rim], up, from_right[:, :rim]], axis=2)
    middle = jnp.concatenate([left, block, right], axis=2)
    bottom = jnp.concatenate([from_left[:, rim:], down, from_right[:, rim:]], axis=2)
    return jnp.concatenate([top, middle, bottom], axis=1)


def fold(canvas, rim):
    full = canvas.shape[1]
    side = full - 2 * rim
    bf = jnp.bfloat16
    lo, hi = slice(0, rim), slice(full - rim, full)
    mid = slice(rim, rim + side)
    to_left = jnp.concatenate([canvas[:, lo, lo], canvas[:, hi, lo]], axis=1).astype(bf)
    to_right = jnp.concatenate([canvas[:, lo, hi], canvas[:, hi, hi]], axis=1).astype(bf)
    got_right = shift(to_left, "visit", -1).astype(jnp.float32)
    got_left = shift(to_right, "visit", 1).astype(jnp.float32)
    top = canvas[:, lo, mid]
    bottom = canvas[:, hi, mid]
    top = top + jnp.concatenate([got_left[:, :rim], got_right[:, :rim]], axis=2)
    bottom = bottom + jnp.concatenate([got_left[:, rim:], got_right[:, rim:]], axis=2)
    from_down = shift(top.astype(bf), "sky", -1).astype(jnp.float32)
    from_up = shift(bottom.astype(bf), "sky", 1).astype(jnp.float32)
    from_right = shift(canvas[:, mid, lo].astype(bf), "visit", -1).astype(jnp.float32)
    from_left = shift(canvas[:, mid, hi].astype(bf), "visit", 1).astype(jnp.float32)
    interior = canvas[:, mid, mid]
    interior = interior.at[:, :rim, :].add(from_up)
    interior = interior.at[:, side - rim :, :].add(from_down)
    interior = interior.at[:, :, :rim].add(from_left)
    interior = interior.at[:, :, side - rim :].add(from_right)
    return interior


def segment_kernel(terms, w_ref, win_ref, obs_ref, rows_ref, rows_t_ref, cols_ref, cols_t_ref,
                   out_ref, acc_ref, res_ref):
    seg = pl.program_id(0)
    f32 = jnp.float32
    acc_ref[...] = jnp.zeros(acc_ref.shape, f32)

    def forward(k, carry):
        left = jnp.dot(rows_ref[k], win_ref[0], preferred_element_type=f32).astype(jnp.bfloat16)
        acc_ref[...] += w_ref[seg, k] * jnp.dot(left, cols_t_ref[k], preferred_element_type=f32)
        return carry

    lax.fori_loop(0, terms, forward, 0)
    res_ref[...] = (acc_ref[...] - obs_ref[0].astype(f32)).astype(jnp.bfloat16)
    acc_ref[...] = jnp.zeros(acc_ref.shape, f32)

    def backward(k, carry):
        right = jnp.dot(res_ref[...], cols_ref[k], preferred_element_type=f32).astype(jnp.bfloat16)
        acc_ref[...] += w_ref[seg, k] * jnp.dot(rows_t_ref[k], right, preferred_element_type=f32)
        return carry

    lax.fori_loop(0, terms, backward, 0)
    out_ref[0] = acc_ref[...].astype(out_ref.dtype)


def adjoints(windows, observed, psf_rows, psf_cols, psf_weights):
    segs, pix, _ = windows.shape
    terms = psf_rows.shape[0]
    rows_t = jnp.swapaxes(psf_rows, 1, 2)
    cols_t = jnp.swapaxes(psf_cols, 1, 2)
    seg_spec = pl.BlockSpec((1, pix, pix), lambda i: (i, 0, 0))
    psf_spec = pl.BlockSpec((terms, pix, pix), lambda i: (0, 0, 0))
    flops = segs * terms * 4 * 2 * pix ** 3
    moved = 2 * pix * pix * (3 * segs + 4 * terms)
    return pl.pallas_call(
        functools.partial(segment_kernel, terms),
        grid=(segs,),
        in_specs=[
            pl.BlockSpec(memory_space=pltpu.SMEM),
            seg_spec,
            seg_spec,
            psf_spec,
            psf_spec,
            psf_spec,
            psf_spec,
        ],
        out_specs=seg_spec,
        out_shape=jax.ShapeDtypeStruct((segs, pix, pix), jnp.bfloat16),
        scratch_shapes=[
            pltpu.VMEM((pix, pix), jnp.float32),
            pltpu.VMEM((pix, pix), jnp.bfloat16),
        ],
        compiler_params=pltpu.CompilerParams(
            dimension_semantics=("arbitrary",), vmem_limit_bytes=56 * 1024 * 1024
        ),
        cost_estimate=pl.CostEstimate(flops=flops, bytes_accessed=moved, transcendentals=0),
    )(psf_weights, windows, observed, psf_rows, rows_t, psf_cols, cols_t)


def per_device(
    sky_image,
    observed,
    footprint,
    segment_band,
    offsets,
    psf_rows,
    psf_cols,
    psf_weights,
    step_sizes,
):
    block_side = sky_image.shape[1]
    pixels = observed.shape[1]
    segs = observed.shape[0]
    rim = (pixels // TILE + 1) // 2 * TILE
    sky_bf = sky_image.astype(jnp.bfloat16)
    extended = halo(sky_bf, rim)
    row_anchor = lax.axis_index("sky") * block_side - rim
    col_anchor = lax.axis_index("visit") * block_side - rim
    top_rows = footprint[:, 0] * TILE + offsets[:, 0] - row_anchor
    left_cols = footprint[:, 1] * TILE + offsets[:, 1] - col_anchor
    windows = jnp.stack(
        [
            lax.dynamic_slice(
                extended, (segment_band[s], top_rows[s], left_cols[s]), (1, pixels, pixels)
            )[0]
            for s in range(segs)
        ]
    )
    adj = adjoints(windows, observed, psf_rows, psf_cols, psf_weights)
    canvas = jnp.zeros(extended.shape, jnp.float32)
    for s in range(segs):
        at = (segment_band[s], top_rows[s], left_cols[s])
        current = lax.dynamic_slice(canvas, at, (1, pixels, pixels))
        canvas = lax.dynamic_update_slice(
            canvas, current + adj[s].astype(jnp.float32)[None], at
        )
    gradient = fold(canvas, rim)
    return sky_image - step_sizes[:, None, None] * gradient


def solution(mesh):
    placed = (
        P(None, "sky", "visit"),
        P(("sky", "visit"), None, None),
        P(("sky", "visit"), None),
        P(("sky", "visit")),
        P(("sky", "visit"), None),
        P(),
        P(),
        P(("sky", "visit"), None),
        P(),
    )
    return jax.shard_map(
        per_device, mesh=mesh, in_specs=placed, out_specs=P(None, "sky", "visit"), check_vma=False
    )
```

```python
import functools

import jax
import jax.numpy as jnp
from jax import lax
from jax.experimental import pallas as pl
from jax.experimental.pallas import tpu as pltpu
from jax.sharding import PartitionSpec as P

TILE = 128


def shift(value, axis, by):
    count = lax.axis_size(axis)
    pairs = [(i, i + by) for i in range(count) if 0 <= i + by < count]
    return lax.ppermute(value, axis, pairs)


def halo(block, rim):
    side = block.shape[1]
    up = shift(block[:, side - rim :, :], "sky", 1)
    down = shift(block[:, :rim, :], "sky", -1)
    left = shift(block[:, :, side - rim :], "visit", 1)
    right = shift(block[:, :, :rim], "visit", -1)
    from_left = shift(
        jnp.concatenate([up[:, :, side - rim :], down[:, :, side - rim :]], axis=1), "visit", 1
    )
    from_right = shift(jnp.concatenate([up[:, :, :rim], down[:, :, :rim]], axis=1), "visit", -1)
    top = jnp.concatenate([from_left[:, :rim], up, from_right[:, :rim]], axis=2)
    middle = jnp.concatenate([left, block, right], axis=2)
    bottom = jnp.concatenate([from_left[:, rim:], down, from_right[:, rim:]], axis=2)
    return jnp.concatenate([top, middle, bottom], axis=1)


def fold(canvas, rim, full):
    side = full - 2 * rim
    bf = jnp.bfloat16
    lo, hi = slice(0, rim), slice(full - rim, full)
    mid = slice(rim, rim + side)
    to_left = jnp.concatenate([canvas[:, lo, lo], canvas[:, hi, lo]], axis=1).astype(bf)
    to_right = jnp.concatenate([canvas[:, lo, hi], canvas[:, hi, hi]], axis=1).astype(bf)
    got_right = shift(to_left, "visit", -1).astype(jnp.float32)
    got_left = shift(to_right, "visit", 1).astype(jnp.float32)
    top = canvas[:, lo, mid]
    bottom = canvas[:, hi, mid]
    top = top + jnp.concatenate([got_left[:, :rim], got_right[:, :rim]], axis=2)
    bottom = bottom + jnp.concatenate([got_left[:, rim:], got_right[:, rim:]], axis=2)
    from_down = shift(top.astype(bf), "sky", -1).astype(jnp.float32)
    from_up = shift(bottom.astype(bf), "sky", 1).astype(jnp.float32)
    from_right = shift(canvas[:, mid, lo].astype(bf), "visit", -1).astype(jnp.float32)
    from_left = shift(canvas[:, mid, hi].astype(bf), "visit", 1).astype(jnp.float32)
    interior = canvas[:, mid, mid]
    interior = interior.at[:, :rim, :].add(from_up)
    interior = interior.at[:, side - rim :, :].add(from_down)
    interior = interior.at[:, :, :rim].add(from_left)
    interior = interior.at[:, :, side - rim :].add(from_right)
    return interior


def segment_kernel(segs, terms, meta_ref, w_ref, win_ref, obs_ref, rows_ref, rows_t_ref, cols_ref,
                   cols_t_ref, canvas_ref, acc_ref, res_ref):
    f32 = jnp.float32
    bf = jnp.bfloat16
    pix = win_ref.shape[1]
    width = canvas_ref.shape[2]
    tall = pix + 8
    canvas_ref[...] = jnp.zeros(canvas_ref.shape, f32)

    def one_segment(s, carry):
        acc_ref[...] = jnp.zeros(acc_ref.shape, f32)

        def forward(k, c):
            left = jnp.dot(rows_ref[k], win_ref[s], preferred_element_type=f32).astype(bf)
            acc_ref[...] += w_ref[s, k] * jnp.dot(left, cols_t_ref[k], preferred_element_type=f32)
            return c

        lax.fori_loop(0, terms, forward, 0)
        res_ref[...] = (acc_ref[...] - obs_ref[s].astype(f32)).astype(bf)
        acc_ref[...] = jnp.zeros(acc_ref.shape, f32)

        def backward(k, c):
            right = jnp.dot(res_ref[...], cols_ref[k], preferred_element_type=f32).astype(bf)
            acc_ref[...] += w_ref[s, k] * jnp.dot(rows_t_ref[k], right, preferred_element_type=f32)
            return c

        lax.fori_loop(0, terms, backward, 0)
        adj = acc_ref[...].astype(bf)
        band = meta_ref[0, s]
        row_base = meta_ref[1, s]
        row_rest = meta_ref[2, s]
        col_at = meta_ref[3, s]
        src_col = lax.broadcasted_iota(jnp.int32, (pix, width), 0)
        dst_col = lax.broadcasted_iota(jnp.int32, (pix, width), 1)
        col_shift = (dst_col == src_col + col_at).astype(bf)
        spread_cols = jnp.dot(adj, col_shift, preferred_element_type=f32).astype(bf)
        dst_row = lax.broadcasted_iota(jnp.int32, (tall, pix), 0)
        src_row = lax.broadcasted_iota(jnp.int32, (tall, pix), 1)
        row_shift = (dst_row == src_row + row_rest).astype(bf)
        placed = jnp.dot(row_shift, spread_cols, preferred_element_type=f32)
        rows_at = pl.ds(pl.multiple_of(row_base, 8), tall)
        canvas_ref[band, rows_at, :] += placed
        return carry

    lax.fori_loop(0, segs, one_segment, 0)


def accumulate(meta, windows, observed, psf_rows, psf_cols, psf_weights, bands, full):
    segs, pix, _ = windows.shape
    terms = psf_rows.shape[0]
    rows_t = jnp.swapaxes(psf_rows, 1, 2)
    cols_t = jnp.swapaxes(psf_cols, 1, 2)
    smem = pl.BlockSpec(memory_space=pltpu.SMEM)
    vmem = pl.BlockSpec(memory_space=pltpu.VMEM)
    flops = segs * (terms * 4 * 2 * pix ** 3 + 2 * pix * pix * full + 2 * (pix + 8) * pix * full)
    moved = 2 * pix * pix * (2 * segs + 4 * terms) + 4 * bands * (full + 8) * full
    return pl.pallas_call(
        functools.partial(segment_kernel, segs, terms),
        in_specs=[smem, smem, vmem, vmem, vmem, vmem, vmem, vmem],
        out_specs=vmem,
        out_shape=jax.ShapeDtypeStruct((bands, full + 8, full), jnp.float32),
        scratch_shapes=[
            pltpu.VMEM((pix, pix), jnp.float32),
            pltpu.VMEM((pix, pix), jnp.bfloat16),
        ],
        compiler_params=pltpu.CompilerParams(vmem_limit_bytes=62 * 1024 * 1024),
        cost_estimate=pl.CostEstimate(flops=flops, bytes_accessed=moved, transcendentals=0),
    )(meta, psf_weights, windows, observed, psf_rows, rows_t, psf_cols, cols_t)


def per_device(
    sky_image,
    observed,
    footprint,
    segment_band,
    offsets,
    psf_rows,
    psf_cols,
    psf_weights,
    step_sizes,
):
    block_side = sky_image.shape[1]
    pixels = observed.shape[1]
    segs = observed.shape[0]
    rim = (pixels // TILE + 1) // 2 * TILE
    sky_bf = sky_image.astype(jnp.bfloat16)
    extended = halo(sky_bf, rim)
    row_anchor = lax.axis_index("sky") * block_side - rim
    col_anchor = lax.axis_index("visit") * block_side - rim
    top_rows = footprint[:, 0] * TILE + offsets[:, 0] - row_anchor
    left_cols = footprint[:, 1] * TILE + offsets[:, 1] - col_anchor
    windows = jnp.stack(
        [
            lax.dynamic_slice(
                extended, (segment_band[s], top_rows[s], left_cols[s]), (1, pixels, pixels)
            )[0]
            for s in range(segs)
        ]
    )
    row_base = top_rows // 8 * 8
    meta = jnp.stack([segment_band, row_base, top_rows - row_base, left_cols]).astype(jnp.int32)
    canvas = accumulate(
        meta, windows, observed, psf_rows, psf_cols, psf_weights, extended.shape[0], extended.shape[1]
    )
    gradient = fold(canvas, rim, extended.shape[1])
    return sky_image - step_sizes[:, None, None] * gradient


def solution(mesh):
    placed = (
        P(None, "sky", "visit"),
        P(("sky", "visit"), None, None),
        P(("sky", "visit"), None),
        P(("sky", "visit")),
        P(("sky", "visit"), None),
        P(),
        P(),
        P(("sky", "visit"), None),
        P(),
    )
    return jax.shard_map(
        per_device, mesh=mesh, in_specs=placed, out_specs=P(None, "sky", "visit"), check_vma=False
    )
```

```python
import functools

import jax
import jax.numpy as jnp
from jax import lax
from jax.experimental import pallas as pl
from jax.experimental.pallas import tpu as pltpu
from jax.sharding import PartitionSpec as P

TILE = 128


def shift(value, axis, by):
    count = lax.axis_size(axis)
    pairs = [(i, i + by) for i in range(count) if 0 <= i + by < count]
    return lax.ppermute(value, axis, pairs)


def halo(block, rim):
    side = block.shape[1]
    up = shift(block[:, side - rim :, :], "sky", 1)
    down = shift(block[:, :rim, :], "sky", -1)
    left = shift(block[:, :, side - rim :], "visit", 1)
    right = shift(block[:, :, :rim], "visit", -1)
    from_left = shift(
        jnp.concatenate([up[:, :, side - rim :], down[:, :, side - rim :]], axis=1), "visit", 1
    )
    from_right = shift(jnp.concatenate([up[:, :, :rim], down[:, :, :rim]], axis=1), "visit", -1)
    top = jnp.concatenate([from_left[:, :rim], up, from_right[:, :rim]], axis=2)
    middle = jnp.concatenate([left, block, right], axis=2)
    bottom = jnp.concatenate([from_left[:, rim:], down, from_right[:, rim:]], axis=2)
    return jnp.concatenate([top, middle, bottom], axis=1)


def fold(canvases, rim, full):
    side = full - 2 * rim
    bf = jnp.bfloat16
    lo, hi = slice(0, rim), slice(full - rim, full)
    mid = slice(rim, rim + side)

    def piece(rs, cs):
        return jnp.stack([c[rs, cs] for c in canvases])

    to_left = jnp.concatenate([piece(lo, lo), piece(hi, lo)], axis=1).astype(bf)
    to_right = jnp.concatenate([piece(lo, hi), piece(hi, hi)], axis=1).astype(bf)
    got_right = shift(to_left, "visit", -1).astype(jnp.float32)
    got_left = shift(to_right, "visit", 1).astype(jnp.float32)
    top = piece(lo, mid)
    bottom = piece(hi, mid)
    top = top + jnp.concatenate([got_left[:, :rim], got_right[:, :rim]], axis=2)
    bottom = bottom + jnp.concatenate([got_left[:, rim:], got_right[:, rim:]], axis=2)
    from_down = shift(top.astype(bf), "sky", -1).astype(jnp.float32)
    from_up = shift(bottom.astype(bf), "sky", 1).astype(jnp.float32)
    from_right = shift(piece(mid, lo).astype(bf), "visit", -1).astype(jnp.float32)
    from_left = shift(piece(mid, hi).astype(bf), "visit", 1).astype(jnp.float32)
    interior = piece(mid, mid)
    interior = interior.at[:, :rim, :].add(from_up)
    interior = interior.at[:, side - rim :, :].add(from_down)
    interior = interior.at[:, :, :rim].add(from_left)
    interior = interior.at[:, :, side - rim :].add(from_right)
    return interior


def band_kernel(segs, terms, band_ref, meta_ref, w_ref, ext_ref, obs_ref, rows_ref, rows_t_ref,
                cols_ref, cols_t_ref, canvas_ref, acc_ref, res_ref, win_ref):
    f32 = jnp.float32
    bf = jnp.bfloat16
    pix = obs_ref.shape[1]
    width = canvas_ref.shape[1]
    tall = pix + 8
    slab_rows = pix + 16
    canvas_ref[...] = jnp.zeros(canvas_ref.shape, f32)

    def one_segment(s, carry):
        @pl.when(meta_ref[0, s] == band_ref[0])
        def _():
            slab = ext_ref[pl.ds(pl.multiple_of(meta_ref[4, s], 16), slab_rows), :]
            src_c = lax.broadcasted_iota(jnp.int32, (width, pix), 0)
            dst_c = lax.broadcasted_iota(jnp.int32, (width, pix), 1)
            pick_cols = (src_c == dst_c + meta_ref[3, s]).astype(bf)
            narrow = jnp.dot(slab, pick_cols, preferred_element_type=f32).astype(bf)
            dst_r = lax.broadcasted_iota(jnp.int32, (pix, slab_rows), 0)
            src_r = lax.broadcasted_iota(jnp.int32, (pix, slab_rows), 1)
            pick_rows = (src_r == dst_r + meta_ref[5, s]).astype(bf)
            win_ref[...] = jnp.dot(pick_rows, narrow, preferred_element_type=f32).astype(bf)
            acc_ref[...] = jnp.zeros(acc_ref.shape, f32)

            def forward(k, c):
                left = jnp.dot(rows_ref[k], win_ref[...], preferred_element_type=f32).astype(bf)
                acc_ref[...] += w_ref[s, k] * jnp.dot(left, cols_t_ref[k], preferred_element_type=f32)
                return c

            lax.fori_loop(0, terms, forward, 0)
            res_ref[...] = (acc_ref[...] - obs_ref[s].astype(f32)).astype(bf)
            acc_ref[...] = jnp.zeros(acc_ref.shape, f32)

            def backward(k, c):
                right = jnp.dot(res_ref[...], cols_ref[k], preferred_element_type=f32).astype(bf)
                acc_ref[...] += w_ref[s, k] * jnp.dot(rows_t_ref[k], right, preferred_element_type=f32)
                return c

            lax.fori_loop(0, terms, backward, 0)
            adj = acc_ref[...].astype(bf)
            src_col = lax.broadcasted_iota(jnp.int32, (pix, width), 0)
            dst_col = lax.broadcasted_iota(jnp.int32, (pix, width), 1)
            col_shift = (dst_col == src_col + meta_ref[3, s]).astype(bf)
            spread_cols = jnp.dot(adj, col_shift, preferred_element_type=f32).astype(bf)
            dst_row = lax.broadcasted_iota(jnp.int32, (tall, pix), 0)
            src_row = lax.broadcasted_iota(jnp.int32, (tall, pix), 1)
            row_shift = (dst_row == src_row + meta_ref[2, s]).astype(bf)
            placed = jnp.dot(row_shift, spread_cols, preferred_element_type=f32)
            rows_at = pl.ds(pl.multiple_of(meta_ref[1, s], 8), tall)
            canvas_ref[rows_at, :] += placed

        return carry

    lax.fori_loop(0, segs, one_segment, 0)


def band_canvas(band_id, meta, ext, observed, psf_rows, rows_t, psf_cols, cols_t, psf_weights):
    segs, pix, _ = observed.shape
    terms = psf_rows.shape[0]
    full = ext.shape[1]
    smem = pl.BlockSpec(memory_space=pltpu.SMEM)
    vmem = pl.BlockSpec(memory_space=pltpu.VMEM)
    per_seg = terms * 4 * 2 * pix ** 3 + 2 * pix * pix * full * 3
    moved = 2 * pix * pix * (segs + 4 * terms) + 2 * ext.size + 4 * (full + 8) * full
    return pl.pallas_call(
        functools.partial(band_kernel, segs, terms),
        in_specs=[smem, smem, smem, vmem, vmem, vmem, vmem, vmem, vmem],
        out_specs=vmem,
        out_shape=jax.ShapeDtypeStruct((full + 8, full), jnp.float32),
        scratch_shapes=[
            pltpu.VMEM((pix, pix), jnp.float32),
            pltpu.VMEM((pix, pix), jnp.bfloat16),
            pltpu.VMEM((pix, pix), jnp.bfloat16),
        ],
        compiler_params=pltpu.CompilerParams(vmem_limit_bytes=48 * 1024 * 1024),
        cost_estimate=pl.CostEstimate(flops=per_seg, bytes_accessed=moved, transcendentals=0),
    )(jnp.full((1,), band_id, jnp.int32), meta, psf_weights, ext, observed, psf_rows, rows_t, psf_cols, cols_t)


def per_device(
    sky_image,
    observed,
    footprint,
    segment_band,
    offsets,
    psf_rows,
    psf_cols,
    psf_weights,
    step_sizes,
):
    bands, block_side, _ = sky_image.shape
    pixels = observed.shape[1]
    rim = (pixels // TILE + 1) // 2 * TILE
    full = block_side + 2 * rim
    sky_bf = sky_image.astype(jnp.bfloat16)
    row_anchor = lax.axis_index("sky") * block_side - rim
    col_anchor = lax.axis_index("visit") * block_side - rim
    top_rows = footprint[:, 0] * TILE + offsets[:, 0] - row_anchor
    left_cols = footprint[:, 1] * TILE + offsets[:, 1] - col_anchor
    base8 = top_rows // 8 * 8
    base16 = top_rows // 16 * 16
    meta = jnp.stack(
        [segment_band, base8, top_rows - base8, left_cols, base16, top_rows - base16]
    ).astype(jnp.int32)
    rows_t = jnp.swapaxes(psf_rows, 1, 2)
    cols_t = jnp.swapaxes(psf_cols, 1, 2)
    canvases = []
    for b in range(bands):
        ext = halo(sky_bf[b : b + 1], rim)[0]
        ext = jnp.concatenate([ext, jnp.zeros((16, full), ext.dtype)], axis=0)
        canvases.append(
            band_canvas(b, meta, ext, observed, psf_rows, rows_t, psf_cols, cols_t, psf_weights)
        )
    gradient = fold(canvases, rim, full)
    return sky_image - step_sizes[:, None, None] * gradient


def solution(mesh):
    placed = (
        P(None, "sky", "visit"),
        P(("sky", "visit"), None, None),
        P(("sky", "visit"), None),
        P(("sky", "visit")),
        P(("sky", "visit"), None),
        P(),
        P(),
        P(("sky", "visit"), None),
        P(),
    )
    return jax.shard_map(
        per_device, mesh=mesh, in_specs=placed, out_specs=P(None, "sky", "visit"), check_vma=False
    )
```

```python
import functools

import jax
import jax.numpy as jnp
from jax import lax
from jax.experimental import pallas as pl
from jax.experimental.pallas import tpu as pltpu
from jax.sharding import PartitionSpec as P

TILE = 128


def shift(value, axis, by):
    count = lax.axis_size(axis)
    pairs = [(i, i + by) for i in range(count) if 0 <= i + by < count]
    return lax.ppermute(value, axis, pairs)


def halo(block, rim):
    for axis, dim in (("sky", 1), ("visit", 2)):
        low = shift(lax.slice_in_dim(block, block.shape[dim] - rim, None, axis=dim), axis, 1)
        high = shift(lax.slice_in_dim(block, 0, rim, axis=dim), axis, -1)
        block = jnp.concatenate([low, block, high], axis=dim)
    return block


def fold(canvas, rims, rim, full):
    side = full - 2 * rim
    bf = jnp.bfloat16
    lo, hi = slice(0, rim), slice(full - rim, full)
    mid = slice(rim, rim + side)
    first, second = slice(0, rim), slice(rim, 2 * rim)
    to_left = jnp.concatenate([rims[:, lo, first], rims[:, hi, first]], axis=1)
    to_right = jnp.concatenate([rims[:, lo, second], rims[:, hi, second]], axis=1)
    got_right = shift(to_left, "visit", -1).astype(jnp.float32)
    got_left = shift(to_right, "visit", 1).astype(jnp.float32)
    top = canvas[:, lo, mid]
    bottom = canvas[:, hi, mid]
    top = top + jnp.concatenate([got_left[:, :rim], got_right[:, :rim]], axis=2)
    bottom = bottom + jnp.concatenate([got_left[:, rim:], got_right[:, rim:]], axis=2)
    from_down = shift(top.astype(bf), "sky", -1).astype(jnp.float32)
    from_up = shift(bottom.astype(bf), "sky", 1).astype(jnp.float32)
    from_right = shift(rims[:, mid, first], "visit", -1).astype(jnp.float32)
    from_left = shift(rims[:, mid, second], "visit", 1).astype(jnp.float32)
    interior = canvas[:, mid, mid]
    interior = interior.at[:, :rim, :].add(from_up)
    interior = interior.at[:, side - rim :, :].add(from_down)
    interior = interior.at[:, :, :rim].add(from_left)
    interior = interior.at[:, :, side - rim :].add(from_right)
    return interior


def segment_kernel(segs, terms, meta_ref, w_ref, win_ref, obs_ref, rows_ref, rows_t_ref, cols_ref,
                   cols_t_ref, canvas_ref, rims_ref, acc_ref, res_ref):
    f32 = jnp.float32
    bf = jnp.bfloat16
    pix = win_ref.shape[1]
    width = canvas_ref.shape[2]
    tall = pix + 8
    canvas_ref[...] = jnp.zeros(canvas_ref.shape, f32)

    def one_segment(s, carry):
        acc_ref[...] = jnp.zeros(acc_ref.shape, f32)

        def forward(k, c):
            left = jnp.dot(rows_ref[k], win_ref[s], preferred_element_type=f32).astype(bf)
            acc_ref[...] += w_ref[s, k] * jnp.dot(left, cols_t_ref[k], preferred_element_type=f32)
            return c

        lax.fori_loop(0, terms, forward, 0)
        res_ref[...] = (acc_ref[...] - obs_ref[s].astype(f32)).astype(bf)
        acc_ref[...] = jnp.zeros(acc_ref.shape, f32)

        def backward(k, c):
            right = jnp.dot(res_ref[...], cols_ref[k], preferred_element_type=f32).astype(bf)
            acc_ref[...] += w_ref[s, k] * jnp.dot(rows_t_ref[k], right, preferred_element_type=f32)
            return c

        lax.fori_loop(0, terms, backward, 0)
        adj = acc_ref[...].astype(bf)
        band = meta_ref[0, s]
        row_base = meta_ref[1, s]
        row_rest = meta_ref[2, s]
        col_at = meta_ref[3, s]
        src_col = lax.broadcasted_iota(jnp.int32, (pix, width), 0)
        dst_col = lax.broadcasted_iota(jnp.int32, (pix, width), 1)
        col_shift = (dst_col == src_col + col_at).astype(bf)
        spread_cols = jnp.dot(adj, col_shift, preferred_element_type=f32).astype(bf)
        dst_row = lax.broadcasted_iota(jnp.int32, (tall, pix), 0)
        src_row = lax.broadcasted_iota(jnp.int32, (tall, pix), 1)
        row_shift = (dst_row == src_row + row_rest).astype(bf)
        placed = jnp.dot(row_shift, spread_cols, preferred_element_type=f32)
        rows_at = pl.ds(pl.multiple_of(row_base, 8), tall)
        canvas_ref[band, rows_at, :] += placed
        return carry

    lax.fori_loop(0, segs, one_segment, 0)
    rim = rims_ref.shape[2] // 2
    rows = rims_ref.shape[1]
    rims_ref[:, :, :rim] = canvas_ref[:, :rows, :rim].astype(rims_ref.dtype)
    rims_ref[:, :, rim:] = canvas_ref[:, :rows, width - rim :].astype(rims_ref.dtype)


def accumulate(meta, windows, observed, psf_rows, psf_cols, psf_weights, bands, full, rim):
    segs, pix, _ = windows.shape
    terms = psf_rows.shape[0]
    rows_t = jnp.swapaxes(psf_rows, 1, 2)
    cols_t = jnp.swapaxes(psf_cols, 1, 2)
    smem = pl.BlockSpec(memory_space=pltpu.SMEM)
    vmem = pl.BlockSpec(memory_space=pltpu.VMEM)
    flops = segs * (terms * 4 * 2 * pix ** 3 + 2 * pix * pix * full + 2 * (pix + 8) * pix * full)
    moved = 2 * pix * pix * (2 * segs + 4 * terms) + 4 * bands * (full + 8) * full
    return pl.pallas_call(
        functools.partial(segment_kernel, segs, terms),
        in_specs=[smem, smem, vmem, vmem, vmem, vmem, vmem, vmem],
        out_specs=(vmem, vmem),
        out_shape=(
            jax.ShapeDtypeStruct((bands, full + 8, full), jnp.float32),
            jax.ShapeDtypeStruct((bands, full, 2 * rim), jnp.bfloat16),
        ),
        scratch_shapes=[
            pltpu.VMEM((pix, pix), jnp.float32),
            pltpu.VMEM((pix, pix), jnp.bfloat16),
        ],
        compiler_params=pltpu.CompilerParams(vmem_limit_bytes=62 * 1024 * 1024),
        cost_estimate=pl.CostEstimate(flops=flops, bytes_accessed=moved, transcendentals=0),
    )(meta, psf_weights, windows, observed, psf_rows, rows_t, psf_cols, cols_t)


def per_device(
    sky_image,
    observed,
    footprint,
    segment_band,
    offsets,
    psf_rows,
    psf_cols,
    psf_weights,
    step_sizes,
):
    block_side = sky_image.shape[1]
    pixels = observed.shape[1]
    segs = observed.shape[0]
    rim = (pixels // TILE + 1) // 2 * TILE
    sky_bf = sky_image.astype(jnp.bfloat16)
    extended = halo(sky_bf, rim)
    row_anchor = lax.axis_index("sky") * block_side - rim
    col_anchor = lax.axis_index("visit") * block_side - rim
    top_rows = footprint[:, 0] * TILE + offsets[:, 0] - row_anchor
    left_cols = footprint[:, 1] * TILE + offsets[:, 1] - col_anchor
    windows = jnp.stack(
        [
            lax.dynamic_slice(
                extended, (segment_band[s], top_rows[s], left_cols[s]), (1, pixels, pixels)
            )[0]
            for s in range(segs)
        ]
    )
    row_base = top_rows // 8 * 8
    meta = jnp.stack([segment_band, row_base, top_rows - row_base, left_cols]).astype(jnp.int32)
    canvas, rims = accumulate(
        meta, windows, observed, psf_rows, psf_cols, psf_weights, extended.shape[0], extended.shape[1],
        rim,
    )
    gradient = fold(canvas, rims, rim, extended.shape[1])
    return sky_image - step_sizes[:, None, None] * gradient


def solution(mesh):
    placed = (
        P(None, "sky", "visit"),
        P(("sky", "visit"), None, None),
        P(("sky", "visit"), None),
        P(("sky", "visit")),
        P(("sky", "visit"), None),
        P(),
        P(),
        P(("sky", "visit"), None),
        P(),
    )
    return jax.shard_map(
        per_device, mesh=mesh, in_specs=placed, out_specs=P(None, "sky", "visit"), check_vma=False
    )
```

```python
import functools

import jax
import jax.numpy as jnp
from jax import lax
from jax.experimental import pallas as pl
from jax.experimental.pallas import tpu as pltpu
from jax.sharding import PartitionSpec as P

TILE = 128


def shift(value, axis, by):
    count = lax.axis_size(axis)
    pairs = [(i, i + by) for i in range(count) if 0 <= i + by < count]
    return lax.ppermute(value, axis, pairs)


def halo(block, rim):
    side = block.shape[1]
    up = shift(block[:, side - rim :, :], "sky", 1)
    down = shift(block[:, :rim, :], "sky", -1)
    left = shift(block[:, :, side - rim :], "visit", 1)
    right = shift(block[:, :, :rim], "visit", -1)
    to_right = jnp.concatenate([up[:, :, side - rim :], down[:, :, side - rim :]], axis=1)
    to_left = jnp.concatenate([up[:, :, :rim], down[:, :, :rim]], axis=1)
    to_right, to_left, left, right = lax.optimization_barrier((to_right, to_left, left, right))
    from_left = shift(to_right, "visit", 1)
    from_right = shift(to_left, "visit", -1)
    top = jnp.concatenate([from_left[:, :rim], up, from_right[:, :rim]], axis=2)
    middle = jnp.concatenate([left, block, right], axis=2)
    bottom = jnp.concatenate([from_left[:, rim:], down, from_right[:, rim:]], axis=2)
    return jnp.concatenate([top, middle, bottom], axis=1)


def fold(canvas, rims, rim, full):
    side = full - 2 * rim
    bf = jnp.bfloat16
    lo, hi = slice(0, rim), slice(full - rim, full)
    mid = slice(rim, rim + side)
    first, second = slice(0, rim), slice(rim, 2 * rim)
    to_left = jnp.concatenate([rims[:, lo, first], rims[:, hi, first]], axis=1)
    to_right = jnp.concatenate([rims[:, lo, second], rims[:, hi, second]], axis=1)
    got_right = shift(to_left, "visit", -1).astype(jnp.float32)
    got_left = shift(to_right, "visit", 1).astype(jnp.float32)
    top = canvas[:, lo, mid]
    bottom = canvas[:, hi, mid]
    top = top + jnp.concatenate([got_left[:, :rim], got_right[:, :rim]], axis=2)
    bottom = bottom + jnp.concatenate([got_left[:, rim:], got_right[:, rim:]], axis=2)
    from_down = shift(top.astype(bf), "sky", -1).astype(jnp.float32)
    from_up = shift(bottom.astype(bf), "sky", 1).astype(jnp.float32)
    from_right = shift(rims[:, mid, first], "visit", -1).astype(jnp.float32)
    from_left = shift(rims[:, mid, second], "visit", 1).astype(jnp.float32)
    interior = canvas[:, mid, mid]
    interior = interior.at[:, :rim, :].add(from_up)
    interior = interior.at[:, side - rim :, :].add(from_down)
    interior = interior.at[:, :, :rim].add(from_left)
    interior = interior.at[:, :, side - rim :].add(from_right)
    return interior


def segment_kernel(segs, terms, meta_ref, w_ref, win_ref, obs_ref, rows_ref, rows_t_ref, cols_ref,
                   cols_t_ref, canvas_ref, rims_ref, acc_ref, res_ref):
    f32 = jnp.float32
    bf = jnp.bfloat16
    pix = win_ref.shape[1]
    width = canvas_ref.shape[2]
    tall = pix + 8
    canvas_ref[...] = jnp.zeros(canvas_ref.shape, f32)

    def one_segment(s, carry):
        acc_ref[...] = jnp.zeros(acc_ref.shape, f32)

        def forward(k, c):
            left = jnp.dot(rows_ref[k], win_ref[s], preferred_element_type=f32).astype(bf)
            acc_ref[...] += w_ref[s, k] * jnp.dot(left, cols_t_ref[k], preferred_element_type=f32)
            return c

        lax.fori_loop(0, terms, forward, 0)
        res_ref[...] = (acc_ref[...] - obs_ref[s].astype(f32)).astype(bf)
        acc_ref[...] = jnp.zeros(acc_ref.shape, f32)

        def backward(k, c):
            right = jnp.dot(res_ref[...], cols_ref[k], preferred_element_type=f32).astype(bf)
            acc_ref[...] += w_ref[s, k] * jnp.dot(rows_t_ref[k], right, preferred_element_type=f32)
            return c

        lax.fori_loop(0, terms, backward, 0)
        adj = acc_ref[...].astype(bf)
        band = meta_ref[0, s]
        row_base = meta_ref[1, s]
        row_rest = meta_ref[2, s]
        col_at = meta_ref[3, s]
        src_col = lax.broadcasted_iota(jnp.int32, (pix, width), 0)
        dst_col = lax.broadcasted_iota(jnp.int32, (pix, width), 1)
        col_shift = (dst_col == src_col + col_at).astype(bf)
        spread_cols = jnp.dot(adj, col_shift, preferred_element_type=f32).astype(bf)
        dst_row = lax.broadcasted_iota(jnp.int32, (tall, pix), 0)
        src_row = lax.broadcasted_iota(jnp.int32, (tall, pix), 1)
        row_shift = (dst_row == src_row + row_rest).astype(bf)
        placed = jnp.dot(row_shift, spread_cols, preferred_element_type=f32)
        rows_at = pl.ds(pl.multiple_of(row_base, 8), tall)
        canvas_ref[band, rows_at, :] += placed
        return carry

    lax.fori_loop(0, segs, one_segment, 0)
    rim = rims_ref.shape[2] // 2
    rows = rims_ref.shape[1]
    rims_ref[:, :, :rim] = canvas_ref[:, :rows, :rim].astype(rims_ref.dtype)
    rims_ref[:, :, rim:] = canvas_ref[:, :rows, width - rim :].astype(rims_ref.dtype)


def accumulate(meta, windows, observed, psf_rows, psf_cols, psf_weights, bands, full, rim):
    segs, pix, _ = windows.shape
    terms = psf_rows.shape[0]
    rows_t = jnp.swapaxes(psf_rows, 1, 2)
    cols_t = jnp.swapaxes(psf_cols, 1, 2)
    smem = pl.BlockSpec(memory_space=pltpu.SMEM)
    vmem = pl.BlockSpec(memory_space=pltpu.VMEM)
    flops = segs * (terms * 4 * 2 * pix ** 3 + 2 * pix * pix * full + 2 * (pix + 8) * pix * full)
    moved = 2 * pix * pix * (2 * segs + 4 * terms) + 4 * bands * (full + 8) * full
    return pl.pallas_call(
        functools.partial(segment_kernel, segs, terms),
        in_specs=[smem, smem, vmem, vmem, vmem, vmem, vmem, vmem],
        out_specs=(vmem, vmem),
        out_shape=(
            jax.ShapeDtypeStruct((bands, full + 8, full), jnp.float32),
            jax.ShapeDtypeStruct((bands, full, 2 * rim), jnp.bfloat16),
        ),
        scratch_shapes=[
            pltpu.VMEM((pix, pix), jnp.float32),
            pltpu.VMEM((pix, pix), jnp.bfloat16),
        ],
        compiler_params=pltpu.CompilerParams(vmem_limit_bytes=62 * 1024 * 1024),
        cost_estimate=pl.CostEstimate(flops=flops, bytes_accessed=moved, transcendentals=0),
    )(meta, psf_weights, windows, observed, psf_rows, rows_t, psf_cols, cols_t)


def per_device(
    sky_image,
    observed,
    footprint,
    segment_band,
    offsets,
    psf_rows,
    psf_cols,
    psf_weights,
    step_sizes,
):
    block_side = sky_image.shape[1]
    pixels = observed.shape[1]
    segs = observed.shape[0]
    rim = (pixels // TILE + 1) // 2 * TILE
    sky_bf = sky_image.astype(jnp.bfloat16)
    extended = halo(sky_bf, rim)
    row_anchor = lax.axis_index("sky") * block_side - rim
    col_anchor = lax.axis_index("visit") * block_side - rim
    top_rows = footprint[:, 0] * TILE + offsets[:, 0] - row_anchor
    left_cols = footprint[:, 1] * TILE + offsets[:, 1] - col_anchor
    windows = jnp.stack(
        [
            lax.dynamic_slice(
                extended, (segment_band[s], top_rows[s], left_cols[s]), (1, pixels, pixels)
            )[0]
            for s in range(segs)
        ]
    )
    row_base = top_rows // 8 * 8
    meta = jnp.stack([segment_band, row_base, top_rows - row_base, left_cols]).astype(jnp.int32)
    canvas, rims = accumulate(
        meta, windows, observed, psf_rows, psf_cols, psf_weights, extended.shape[0], extended.shape[1],
        rim,
    )
    gradient = fold(canvas, rims, rim, extended.shape[1])
    return sky_image - step_sizes[:, None, None] * gradient


def solution(mesh):
    placed = (
        P(None, "sky", "visit"),
        P(("sky", "visit"), None, None),
        P(("sky", "visit"), None),
        P(("sky", "visit")),
        P(("sky", "visit"), None),
        P(),
        P(),
        P(("sky", "visit"), None),
        P(),
    )
    return jax.shard_map(
        per_device, mesh=mesh, in_specs=placed, out_specs=P(None, "sky", "visit"), check_vma=False
    )
```

```python
import functools

import jax
import jax.numpy as jnp
from jax import lax
from jax.experimental import pallas as pl
from jax.experimental.pallas import tpu as pltpu
from jax.sharding import PartitionSpec as P

TILE = 128


def shift(value, axis, by):
    count = lax.axis_size(axis)
    pairs = [(i, i + by) for i in range(count) if 0 <= i + by < count]
    return lax.ppermute(value, axis, pairs)


def halo(block, rim):
    side = block.shape[1]
    up = shift(block[:, side - rim :, :], "sky", 1)
    down = shift(block[:, :rim, :], "sky", -1)
    left = shift(block[:, :, side - rim :], "visit", 1)
    right = shift(block[:, :, :rim], "visit", -1)
    to_right = jnp.concatenate([up[:, :, side - rim :], down[:, :, side - rim :]], axis=1)
    to_left = jnp.concatenate([up[:, :, :rim], down[:, :, :rim]], axis=1)
    to_right, to_left, left, right = lax.optimization_barrier((to_right, to_left, left, right))
    from_left = shift(to_right, "visit", 1)
    from_right = shift(to_left, "visit", -1)
    top = jnp.concatenate([from_left[:, :rim], up, from_right[:, :rim]], axis=2)
    middle = jnp.concatenate([left, block, right], axis=2)
    bottom = jnp.concatenate([from_left[:, rim:], down, from_right[:, rim:]], axis=2)
    pad = jnp.zeros((block.shape[0], 16, top.shape[2]), block.dtype)
    return jnp.concatenate([top, middle, bottom, pad], axis=1)


def fold(canvas, rims, rim, full):
    side = full - 2 * rim
    bf = jnp.bfloat16
    lo, hi = slice(0, rim), slice(full - rim, full)
    mid = slice(rim, rim + side)
    first, second = slice(0, rim), slice(rim, 2 * rim)
    to_left = jnp.concatenate([rims[:, lo, first], rims[:, hi, first]], axis=1)
    to_right = jnp.concatenate([rims[:, lo, second], rims[:, hi, second]], axis=1)
    got_right = shift(to_left, "visit", -1).astype(jnp.float32)
    got_left = shift(to_right, "visit", 1).astype(jnp.float32)
    top = canvas[:, lo, mid]
    bottom = canvas[:, hi, mid]
    top = top + jnp.concatenate([got_left[:, :rim], got_right[:, :rim]], axis=2)
    bottom = bottom + jnp.concatenate([got_left[:, rim:], got_right[:, rim:]], axis=2)
    from_down = shift(top.astype(bf), "sky", -1).astype(jnp.float32)
    from_up = shift(bottom.astype(bf), "sky", 1).astype(jnp.float32)
    from_right = shift(rims[:, mid, first], "visit", -1).astype(jnp.float32)
    from_left = shift(rims[:, mid, second], "visit", 1).astype(jnp.float32)
    interior = canvas[:, mid, mid]
    interior = interior.at[:, :rim, :].add(from_up)
    interior = interior.at[:, side - rim :, :].add(from_down)
    interior = interior.at[:, :, :rim].add(from_left)
    interior = interior.at[:, :, side - rim :].add(from_right)
    return interior


def segment_kernel(segs, terms, rim, foot_ref, off_ref, band_ref, w_ref, ext_ref, obs_ref, rows_ref,
                   rows_t_ref, cols_ref, cols_t_ref, canvas_ref, rims_ref, acc_ref, res_ref, win_ref,
                   slab_ref, sem):
    f32 = jnp.float32
    bf = jnp.bfloat16
    pix = obs_ref.shape[1]
    width = canvas_ref.shape[2]
    tall = pix + 8
    slab_rows = slab_ref.shape[0]
    tile = 128
    row_anchor = lax.axis_index("sky") * pix - rim
    col_anchor = lax.axis_index("visit") * pix - rim
    canvas_ref[...] = jnp.zeros(canvas_ref.shape, f32)

    def one_segment(s, carry):
        band = band_ref[s]
        top = foot_ref[s, 0] * tile + off_ref[s, 0] - row_anchor
        left_at = foot_ref[s, 1] * tile + off_ref[s, 1] - col_anchor
        base16 = lax.shift_left(lax.shift_right_logical(top, 4), 4)
        base8 = lax.shift_left(lax.shift_right_logical(top, 3), 3)
        fetch = pltpu.make_async_copy(
            ext_ref.at[band, pl.ds(pl.multiple_of(base16, 16), slab_rows), :], slab_ref, sem
        )
        fetch.start()
        fetch.wait()
        src_c = lax.broadcasted_iota(jnp.int32, (width, pix), 0)
        dst_c = lax.broadcasted_iota(jnp.int32, (width, pix), 1)
        pick_cols = (src_c == dst_c + left_at).astype(bf)
        narrow = jnp.dot(slab_ref[...], pick_cols, preferred_element_type=f32).astype(bf)
        dst_r = lax.broadcasted_iota(jnp.int32, (pix, slab_rows), 0)
        src_r = lax.broadcasted_iota(jnp.int32, (pix, slab_rows), 1)
        pick_rows = (src_r == dst_r + (top - base16)).astype(bf)
        win_ref[...] = jnp.dot(pick_rows, narrow, preferred_element_type=f32).astype(bf)
        acc_ref[...] = jnp.zeros(acc_ref.shape, f32)

        def forward(k, c):
            left = jnp.dot(rows_ref[k], win_ref[...], preferred_element_type=f32).astype(bf)
            acc_ref[...] += w_ref[s, k] * jnp.dot(left, cols_t_ref[k], preferred_element_type=f32)
            return c

        lax.fori_loop(0, terms, forward, 0)
        res_ref[...] = (acc_ref[...] - obs_ref[s].astype(f32)).astype(bf)
        acc_ref[...] = jnp.zeros(acc_ref.shape, f32)

        def backward(k, c):
            right = jnp.dot(res_ref[...], cols_ref[k], preferred_element_type=f32).astype(bf)
            acc_ref[...] += w_ref[s, k] * jnp.dot(rows_t_ref[k], right, preferred_element_type=f32)
            return c

        lax.fori_loop(0, terms, backward, 0)
        adj = acc_ref[...].astype(bf)
        src_col = lax.broadcasted_iota(jnp.int32, (pix, width), 0)
        dst_col = lax.broadcasted_iota(jnp.int32, (pix, width), 1)
        col_shift = (dst_col == src_col + left_at).astype(bf)
        spread_cols = jnp.dot(adj, col_shift, preferred_element_type=f32).astype(bf)
        dst_row = lax.broadcasted_iota(jnp.int32, (tall, pix), 0)
        src_row = lax.broadcasted_iota(jnp.int32, (tall, pix), 1)
        row_shift = (dst_row == src_row + (top - base8)).astype(bf)
        placed = jnp.dot(row_shift, spread_cols, preferred_element_type=f32)
        rows_at = pl.ds(pl.multiple_of(base8, 8), tall)
        canvas_ref[band, rows_at, :] += placed
        return carry

    lax.fori_loop(0, segs, one_segment, 0)
    half = rims_ref.shape[2] // 2
    rows = rims_ref.shape[1]
    rims_ref[:, :, :half] = canvas_ref[:, :rows, :half].astype(rims_ref.dtype)
    rims_ref[:, :, half:] = canvas_ref[:, :rows, width - half :].astype(rims_ref.dtype)


def accumulate(extended, observed, footprint, offsets, segment_band, psf_rows, psf_cols,
               psf_weights, rim):
    segs, pix, _ = observed.shape
    terms = psf_rows.shape[0]
    bands, _, full = extended.shape
    rows_t = jnp.swapaxes(psf_rows, 1, 2)
    cols_t = jnp.swapaxes(psf_cols, 1, 2)
    smem = pl.BlockSpec(memory_space=pltpu.SMEM)
    vmem = pl.BlockSpec(memory_space=pltpu.VMEM)
    anywhere = pl.BlockSpec(memory_space=pl.ANY)
    flops = segs * (terms * 4 * 2 * pix ** 3 + 6 * pix * pix * full)
    moved = 2 * pix * pix * (3 * segs + 4 * terms) + 4 * bands * (full + 8) * full
    return pl.pallas_call(
        functools.partial(segment_kernel, segs, terms, rim),
        in_specs=[smem, smem, smem, smem, anywhere, vmem, vmem, vmem, vmem, vmem],
        out_specs=(vmem, vmem),
        out_shape=(
            jax.ShapeDtypeStruct((bands, full + 8, full), jnp.float32),
            jax.ShapeDtypeStruct((bands, full, 2 * rim), jnp.bfloat16),
        ),
        scratch_shapes=[
            pltpu.VMEM((pix, pix), jnp.float32),
            pltpu.VMEM((pix, pix), jnp.bfloat16),
            pltpu.VMEM((pix, pix), jnp.bfloat16),
            pltpu.VMEM((pix + 16, full), jnp.bfloat16),
            pltpu.SemaphoreType.DMA(()),
        ],
        compiler_params=pltpu.CompilerParams(vmem_limit_bytes=62 * 1024 * 1024),
        cost_estimate=pl.CostEstimate(flops=flops, bytes_accessed=moved, transcendentals=0),
    )(footprint, offsets, segment_band, psf_weights, extended, observed, psf_rows, rows_t,
      psf_cols, cols_t)


def per_device(
    sky_image,
    observed,
    footprint,
    segment_band,
    offsets,
    psf_rows,
    psf_cols,
    psf_weights,
    step_sizes,
):
    pixels = observed.shape[1]
    rim = (pixels // TILE + 1) // 2 * TILE
    extended = halo(sky_image.astype(jnp.bfloat16), rim)
    canvas, rims = accumulate(
        extended, observed, footprint, offsets, segment_band, psf_rows, psf_cols, psf_weights, rim
    )
    gradient = fold(canvas, rims, rim, extended.shape[2])
    return sky_image - step_sizes[:, None, None] * gradient


def solution(mesh):
    placed = (
        P(None, "sky", "visit"),
        P(("sky", "visit"), None, None),
        P(("sky", "visit"), None),
        P(("sky", "visit")),
        P(("sky", "visit"), None),
        P(),
        P(),
        P(("sky", "visit"), None),
        P(),
    )
    return jax.shard_map(
        per_device, mesh=mesh, in_specs=placed, out_specs=P(None, "sky", "visit"), check_vma=False
    )
```

```python
import functools

import jax
import jax.numpy as jnp
from jax import lax
from jax.experimental import pallas as pl
from jax.experimental.pallas import tpu as pltpu
from jax.sharding import PartitionSpec as P

TILE = 128


def shift(value, axis, by):
    count = lax.axis_size(axis)
    pairs = [(i, i + by) for i in range(count) if 0 <= i + by < count]
    return lax.ppermute(value, axis, pairs)


def halo(block, rim):
    side = block.shape[1]
    up = shift(block[:, side - rim :, :], "sky", 1)
    down = shift(block[:, :rim, :], "sky", -1)
    left = shift(block[:, :, side - rim :], "visit", 1)
    right = shift(block[:, :, :rim], "visit", -1)
    to_right = jnp.concatenate([up[:, :, side - rim :], down[:, :, side - rim :]], axis=1)
    to_left = jnp.concatenate([up[:, :, :rim], down[:, :, :rim]], axis=1)
    to_right, to_left, left, right = lax.optimization_barrier((to_right, to_left, left, right))
    from_left = shift(to_right, "visit", 1)
    from_right = shift(to_left, "visit", -1)
    top = jnp.concatenate([from_left[:, :rim], up, from_right[:, :rim]], axis=2)
    middle = jnp.concatenate([left, block, right], axis=2)
    bottom = jnp.concatenate([from_left[:, rim:], down, from_right[:, rim:]], axis=2)
    return jnp.concatenate([top, middle, bottom], axis=1)


def fold(canvas, rims, rim, full):
    side = full - 2 * rim
    bf = jnp.bfloat16
    lo, hi = slice(0, rim), slice(full - rim, full)
    mid = slice(rim, rim + side)
    first, second = slice(0, rim), slice(rim, 2 * rim)
    to_left = jnp.concatenate([rims[:, lo, first], rims[:, hi, first]], axis=1)
    to_right = jnp.concatenate([rims[:, lo, second], rims[:, hi, second]], axis=1)
    got_right = shift(to_left, "visit", -1).astype(jnp.float32)
    got_left = shift(to_right, "visit", 1).astype(jnp.float32)
    top = canvas[:, lo, mid]
    bottom = canvas[:, hi, mid]
    top = top + jnp.concatenate([got_left[:, :rim], got_right[:, :rim]], axis=2)
    bottom = bottom + jnp.concatenate([got_left[:, rim:], got_right[:, rim:]], axis=2)
    from_down = shift(top.astype(bf), "sky", -1).astype(jnp.float32)
    from_up = shift(bottom.astype(bf), "sky", 1).astype(jnp.float32)
    from_right = shift(rims[:, mid, first], "visit", -1).astype(jnp.float32)
    from_left = shift(rims[:, mid, second], "visit", 1).astype(jnp.float32)
    interior = canvas[:, mid, mid]
    interior = interior.at[:, :rim, :].add(from_up)
    interior = interior.at[:, side - rim :, :].add(from_down)
    interior = interior.at[:, :, :rim].add(from_left)
    interior = interior.at[:, :, side - rim :].add(from_right)
    return interior


def segment_kernel(segs, terms, rim, foot_ref, off_ref, band_ref, w_ref, win_ref, obs_ref, rows_ref,
                   rows_t_ref, cols_ref, cols_t_ref, canvas_ref, rims_ref, acc_ref, res_ref):
    f32 = jnp.float32
    bf = jnp.bfloat16
    pix = obs_ref.shape[1]
    width = canvas_ref.shape[2]
    tall = pix + 8
    tile = 128
    row_anchor = lax.axis_index("sky") * pix - rim
    col_anchor = lax.axis_index("visit") * pix - rim
    canvas_ref[...] = jnp.zeros(canvas_ref.shape, f32)

    def one_segment(s, carry):
        band = band_ref[s]
        top = foot_ref[s, 0] * tile + off_ref[s, 0] - row_anchor
        left_at = foot_ref[s, 1] * tile + off_ref[s, 1] - col_anchor
        base8 = lax.shift_left(lax.shift_right_logical(top, 3), 3)
        acc_ref[...] = jnp.zeros(acc_ref.shape, f32)

        def forward(k, c):
            left = jnp.dot(rows_ref[k], win_ref[s], preferred_element_type=f32).astype(bf)
            acc_ref[...] += w_ref[s, k] * jnp.dot(left, cols_t_ref[k], preferred_element_type=f32)
            return c

        lax.fori_loop(0, terms, forward, 0)
        res_ref[...] = (acc_ref[...] - obs_ref[s].astype(f32)).astype(bf)
        acc_ref[...] = jnp.zeros(acc_ref.shape, f32)

        def backward(k, c):
            right = jnp.dot(res_ref[...], cols_ref[k], preferred_element_type=f32).astype(bf)
            acc_ref[...] += w_ref[s, k] * jnp.dot(rows_t_ref[k], right, preferred_element_type=f32)
            return c

        lax.fori_loop(0, terms, backward, 0)
        adj = acc_ref[...].astype(bf)
        src_col = lax.broadcasted_iota(jnp.int32, (pix, width), 0)
        dst_col = lax.broadcasted_iota(jnp.int32, (pix, width), 1)
        col_shift = (dst_col == src_col + left_at).astype(bf)
        spread_cols = jnp.dot(adj, col_shift, preferred_element_type=f32).astype(bf)
        dst_row = lax.broadcasted_iota(jnp.int32, (tall, pix), 0)
        src_row = lax.broadcasted_iota(jnp.int32, (tall, pix), 1)
        row_shift = (dst_row == src_row + (top - base8)).astype(bf)
        placed = jnp.dot(row_shift, spread_cols, preferred_element_type=f32)
        rows_at = pl.ds(pl.multiple_of(base8, 8), tall)
        canvas_ref[band, rows_at, :] += placed
        return carry

    lax.fori_loop(0, segs, one_segment, 0)
    half = rims_ref.shape[2] // 2
    rows = rims_ref.shape[1]
    rims_ref[:, :, :half] = canvas_ref[:, :rows, :half].astype(rims_ref.dtype)
    rims_ref[:, :, half:] = canvas_ref[:, :rows, width - half :].astype(rims_ref.dtype)


def accumulate(windows, observed, footprint, offsets, segment_band, psf_rows, psf_cols,
               psf_weights, rim, extended_shape):
    segs, pix, _ = observed.shape
    terms = psf_rows.shape[0]
    bands, full, _ = extended_shape
    rows_t = jnp.swapaxes(psf_rows, 1, 2)
    cols_t = jnp.swapaxes(psf_cols, 1, 2)
    smem = pl.BlockSpec(memory_space=pltpu.SMEM)
    vmem = pl.BlockSpec(memory_space=pltpu.VMEM)
    flops = segs * (terms * 4 * 2 * pix ** 3 + 6 * pix * pix * full)
    moved = 2 * pix * pix * (3 * segs + 4 * terms) + 4 * bands * (full + 8) * full
    return pl.pallas_call(
        functools.partial(segment_kernel, segs, terms, rim),
        in_specs=[smem, smem, smem, smem, vmem, vmem, vmem, vmem, vmem, vmem],
        out_specs=(vmem, vmem),
        out_shape=(
            jax.ShapeDtypeStruct((bands, full + 8, full), jnp.float32),
            jax.ShapeDtypeStruct((bands, full, 2 * rim), jnp.bfloat16),
        ),
        scratch_shapes=[
            pltpu.VMEM((pix, pix), jnp.float32),
            pltpu.VMEM((pix, pix), jnp.bfloat16),
        ],
        compiler_params=pltpu.CompilerParams(vmem_limit_bytes=62 * 1024 * 1024),
        cost_estimate=pl.CostEstimate(flops=flops, bytes_accessed=moved, transcendentals=0),
    )(footprint, offsets, segment_band, psf_weights, windows, observed, psf_rows, rows_t,
      psf_cols, cols_t)


def per_device(
    sky_image,
    observed,
    footprint,
    segment_band,
    offsets,
    psf_rows,
    psf_cols,
    psf_weights,
    step_sizes,
):
    pixels = observed.shape[1]
    rim = (pixels // TILE + 1) // 2 * TILE
    block_side = sky_image.shape[1]
    segs = observed.shape[0]
    sky_bf = sky_image.astype(jnp.bfloat16)
    row_anchor = lax.axis_index("sky") * block_side - rim
    col_anchor = lax.axis_index("visit") * block_side - rim
    top_rows = footprint[:, 0] * TILE + offsets[:, 0] - row_anchor
    left_cols = footprint[:, 1] * TILE + offsets[:, 1] - col_anchor
    at = [(segment_band[s], top_rows[s], left_cols[s]) for s in range(segs)]
    at, sky_bf = lax.optimization_barrier((at, sky_bf))
    extended = halo(sky_bf, rim)
    windows = jnp.stack(
        [lax.dynamic_slice(extended, at[s], (1, pixels, pixels))[0] for s in range(segs)]
    )
    canvas, rims = accumulate(
        windows, observed, footprint, offsets, segment_band, psf_rows, psf_cols, psf_weights, rim,
        extended.shape,
    )
    gradient = fold(canvas, rims, rim, extended.shape[2])
    return sky_image - step_sizes[:, None, None] * gradient


def solution(mesh):
    placed = (
        P(None, "sky", "visit"),
        P(("sky", "visit"), None, None),
        P(("sky", "visit"), None),
        P(("sky", "visit")),
        P(("sky", "visit"), None),
        P(),
        P(),
        P(("sky", "visit"), None),
        P(),
    )
    return jax.shard_map(
        per_device, mesh=mesh, in_specs=placed, out_specs=P(None, "sky", "visit"), check_vma=False
    )
```

```python
import functools

import jax
import jax.numpy as jnp
from jax import lax
from jax.experimental import pallas as pl
from jax.experimental.pallas import tpu as pltpu
from jax.sharding import PartitionSpec as P

TILE = 128


def shift(value, axis, by):
    count = lax.axis_size(axis)
    pairs = [(i, i + by) for i in range(count) if 0 <= i + by < count]
    return lax.ppermute(value, axis, pairs)


def halo(block, rim):
    side = block.shape[1]
    up = shift(block[:, side - rim :, :], "sky", 1)
    down = shift(block[:, :rim, :], "sky", -1)
    left = shift(block[:, :, side - rim :], "visit", 1)
    right = shift(block[:, :, :rim], "visit", -1)
    to_right = jnp.concatenate([up[:, :, side - rim :], down[:, :, side - rim :]], axis=1)
    to_left = jnp.concatenate([up[:, :, :rim], down[:, :, :rim]], axis=1)
    to_right, to_left, left, right = lax.optimization_barrier((to_right, to_left, left, right))
    from_left = shift(to_right, "visit", 1)
    from_right = shift(to_left, "visit", -1)
    top = jnp.concatenate([from_left[:, :rim], up, from_right[:, :rim]], axis=2)
    middle = jnp.concatenate([left, block, right], axis=2)
    bottom = jnp.concatenate([from_left[:, rim:], down, from_right[:, rim:]], axis=2)
    return jnp.concatenate([top, middle, bottom], axis=1)


def fold(canvas, rims, rim, full):
    side = full - 2 * rim
    bf = jnp.bfloat16
    lo, hi = slice(0, rim), slice(full - rim, full)
    mid = slice(rim, rim + side)
    first, second = slice(0, rim), slice(rim, 2 * rim)
    to_left = jnp.concatenate([rims[:, lo, first], rims[:, hi, first]], axis=1)
    to_right = jnp.concatenate([rims[:, lo, second], rims[:, hi, second]], axis=1)
    got_right = shift(to_left, "visit", -1).astype(jnp.float32)
    got_left = shift(to_right, "visit", 1).astype(jnp.float32)
    top = canvas[:, lo, mid]
    bottom = canvas[:, hi, mid]
    top = top + jnp.concatenate([got_left[:, :rim], got_right[:, :rim]], axis=2)
    bottom = bottom + jnp.concatenate([got_left[:, rim:], got_right[:, rim:]], axis=2)
    from_down = shift(top.astype(bf), "sky", -1).astype(jnp.float32)
    from_up = shift(bottom.astype(bf), "sky", 1).astype(jnp.float32)
    from_right = shift(rims[:, mid, first], "visit", -1).astype(jnp.float32)
    from_left = shift(rims[:, mid, second], "visit", 1).astype(jnp.float32)
    interior = canvas[:, mid, mid]
    interior = interior.at[:, :rim, :].add(from_up)
    interior = interior.at[:, side - rim :, :].add(from_down)
    interior = interior.at[:, :, :rim].add(from_left)
    interior = interior.at[:, :, side - rim :].add(from_right)
    return interior


def segment_kernel(segs, terms, rim, foot_ref, off_ref, band_ref, w_ref, win_ref, obs_ref, rows_ref,
                   rows_t_ref, cols_ref, cols_t_ref, canvas_ref, rims_ref, acc_ref, res_ref):
    f32 = jnp.float32
    bf = jnp.bfloat16
    pix = obs_ref.shape[1]
    width = canvas_ref.shape[2]
    tall = pix + 8
    tile = 128
    row_anchor = lax.axis_index("sky") * pix - rim
    col_anchor = lax.axis_index("visit") * pix - rim
    canvas_ref[...] = jnp.zeros(canvas_ref.shape, f32)

    def one_segment(s, carry):
        band = band_ref[s]
        top = foot_ref[s, 0] * tile + off_ref[s, 0] - row_anchor
        left_at = foot_ref[s, 1] * tile + off_ref[s, 1] - col_anchor
        base8 = lax.shift_left(lax.shift_right_logical(top, 3), 3)
        acc_ref[...] = jnp.zeros(acc_ref.shape, f32)

        def forward(k, c):
            left = jnp.dot(rows_ref[k], win_ref[s], preferred_element_type=f32).astype(bf)
            acc_ref[...] += w_ref[s, k] * jnp.dot(left, cols_t_ref[k], preferred_element_type=f32)
            return c

        lax.fori_loop(0, terms, forward, 0)
        res_ref[...] = (acc_ref[...] - obs_ref[s].astype(f32)).astype(bf)
        acc_ref[...] = jnp.zeros(acc_ref.shape, f32)

        def backward(k, c):
            right = jnp.dot(res_ref[...], cols_ref[k], preferred_element_type=f32).astype(bf)
            acc_ref[...] += w_ref[s, k] * jnp.dot(rows_t_ref[k], right, preferred_element_type=f32)
            return c

        lax.fori_loop(0, terms, backward, 0)
        adj = acc_ref[...].astype(bf)
        src_col = lax.broadcasted_iota(jnp.int32, (pix, width), 0)
        dst_col = lax.broadcasted_iota(jnp.int32, (pix, width), 1)
        col_shift = (dst_col == src_col + left_at).astype(bf)
        spread_cols = jnp.dot(adj, col_shift, preferred_element_type=f32).astype(bf)
        dst_row = lax.broadcasted_iota(jnp.int32, (tall, pix), 0)
        src_row = lax.broadcasted_iota(jnp.int32, (tall, pix), 1)
        row_shift = (dst_row == src_row + (top - base8)).astype(bf)
        placed = jnp.dot(row_shift, spread_cols, preferred_element_type=f32)
        rows_at = pl.ds(pl.multiple_of(base8, 8), tall)
        canvas_ref[band, rows_at, :] += placed
        return carry

    lax.fori_loop(0, segs, one_segment, 0)
    half = rims_ref.shape[2] // 2
    rows = rims_ref.shape[1]
    rims_ref[:, :, :half] = canvas_ref[:, :rows, :half].astype(rims_ref.dtype)
    rims_ref[:, :, half:] = canvas_ref[:, :rows, width - half :].astype(rims_ref.dtype)


def accumulate(windows, observed, footprint, offsets, segment_band, psf_rows, psf_cols,
               psf_weights, rim, extended_shape):
    segs, pix, _ = observed.shape
    terms = psf_rows.shape[0]
    bands, full, _ = extended_shape
    rows_t = jnp.swapaxes(psf_rows, 1, 2)
    cols_t = jnp.swapaxes(psf_cols, 1, 2)
    smem = pl.BlockSpec(memory_space=pltpu.SMEM)
    vmem = pl.BlockSpec(memory_space=pltpu.VMEM)
    flops = segs * (terms * 4 * 2 * pix ** 3 + 6 * pix * pix * full)
    moved = 2 * pix * pix * (3 * segs + 4 * terms) + 4 * bands * (full + 8) * full
    return pl.pallas_call(
        functools.partial(segment_kernel, segs, terms, rim),
        in_specs=[smem, smem, smem, smem, vmem, vmem, vmem, vmem, vmem, vmem],
        out_specs=(vmem, vmem),
        out_shape=(
            jax.ShapeDtypeStruct((bands, full + 8, full), jnp.float32),
            jax.ShapeDtypeStruct((bands, full, 2 * rim), jnp.bfloat16),
        ),
        scratch_shapes=[
            pltpu.VMEM((pix, pix), jnp.float32),
            pltpu.VMEM((pix, pix), jnp.bfloat16),
        ],
        compiler_params=pltpu.CompilerParams(vmem_limit_bytes=62 * 1024 * 1024),
        cost_estimate=pl.CostEstimate(flops=flops, bytes_accessed=moved, transcendentals=0),
    )(footprint, offsets, segment_band, psf_weights, windows, observed, psf_rows, rows_t,
      psf_cols, cols_t)


def per_device(
    sky_image,
    observed,
    footprint,
    segment_band,
    offsets,
    psf_rows,
    psf_cols,
    psf_weights,
    step_sizes,
):
    pixels = observed.shape[1]
    rim = (pixels // TILE + 1) // 2 * TILE
    block_side = sky_image.shape[1]
    segs = observed.shape[0]
    sky_bf = sky_image.astype(jnp.bfloat16)
    row_anchor = lax.axis_index("sky") * block_side - rim
    col_anchor = lax.axis_index("visit") * block_side - rim
    top_rows = footprint[:, 0] * TILE + offsets[:, 0] - row_anchor
    left_cols = footprint[:, 1] * TILE + offsets[:, 1] - col_anchor
    at = [(segment_band[s], top_rows[s], left_cols[s]) for s in range(segs)]
    at, sky_bf = lax.optimization_barrier((at, sky_bf))
    extended = halo(sky_bf, rim)
    windows = jnp.stack(
        [
            lax.dynamic_slice(
                extended, at[s], (1, pixels, pixels), allow_negative_indices=False
            )[0]
            for s in range(segs)
        ]
    )
    canvas, rims = accumulate(
        windows, observed, footprint, offsets, segment_band, psf_rows, psf_cols, psf_weights, rim,
        extended.shape,
    )
    gradient = fold(canvas, rims, rim, extended.shape[2])
    return sky_image - step_sizes[:, None, None] * gradient


def solution(mesh):
    placed = (
        P(None, "sky", "visit"),
        P(("sky", "visit"), None, None),
        P(("sky", "visit"), None),
        P(("sky", "visit")),
        P(("sky", "visit"), None),
        P(),
        P(),
        P(("sky", "visit"), None),
        P(),
    )
    return jax.shard_map(
        per_device, mesh=mesh, in_specs=placed, out_specs=P(None, "sky", "visit"), check_vma=False
    )
```

```python
import functools

import jax
import jax.numpy as jnp
from jax import lax
from jax.experimental import pallas as pl
from jax.experimental.pallas import tpu as pltpu
from jax.sharding import PartitionSpec as P

TILE = 128


def shift(value, axis, by):
    count = lax.axis_size(axis)
    pairs = [(i, i + by) for i in range(count) if 0 <= i + by < count]
    return lax.ppermute(value, axis, pairs)


def halo(block, rim):
    side = block.shape[1]
    up = shift(block[:, side - rim :, :], "sky", 1)
    down = shift(block[:, :rim, :], "sky", -1)
    left = shift(block[:, :, side - rim :], "visit", 1)
    right = shift(block[:, :, :rim], "visit", -1)
    to_right = jnp.concatenate([up[:, :, side - rim :], down[:, :, side - rim :]], axis=1)
    to_left = jnp.concatenate([up[:, :, :rim], down[:, :, :rim]], axis=1)
    to_right, to_left, left, right = lax.optimization_barrier((to_right, to_left, left, right))
    from_left = shift(to_right, "visit", 1)
    from_right = shift(to_left, "visit", -1)
    top = jnp.concatenate([from_left[:, :rim], up, from_right[:, :rim]], axis=2)
    middle = jnp.concatenate([left, block, right], axis=2)
    bottom = jnp.concatenate([from_left[:, rim:], down, from_right[:, rim:]], axis=2)
    return jnp.concatenate([top, middle, bottom], axis=1)


def fold(canvas, rims, rim, full):
    side = full - 2 * rim
    bf = jnp.bfloat16
    lo, hi = slice(0, rim), slice(full - rim, full)
    mid = slice(rim, rim + side)
    first, second = slice(0, rim), slice(rim, 2 * rim)
    to_left = jnp.concatenate([rims[:, lo, first], rims[:, hi, first]], axis=1)
    to_right = jnp.concatenate([rims[:, lo, second], rims[:, hi, second]], axis=1)
    got_right = shift(to_left, "visit", -1).astype(jnp.float32)
    got_left = shift(to_right, "visit", 1).astype(jnp.float32)
    top = canvas[:, lo, mid]
    bottom = canvas[:, hi, mid]
    top = top + jnp.concatenate([got_left[:, :rim], got_right[:, :rim]], axis=2)
    bottom = bottom + jnp.concatenate([got_left[:, rim:], got_right[:, rim:]], axis=2)
    from_down = shift(top.astype(bf), "sky", -1).astype(jnp.float32)
    from_up = shift(bottom.astype(bf), "sky", 1).astype(jnp.float32)
    from_right = shift(rims[:, mid, first], "visit", -1).astype(jnp.float32)
    from_left = shift(rims[:, mid, second], "visit", 1).astype(jnp.float32)
    interior = canvas[:, mid, mid]
    interior = interior.at[:, :rim, :].add(from_up)
    interior = interior.at[:, side - rim :, :].add(from_down)
    interior = interior.at[:, :, :rim].add(from_left)
    interior = interior.at[:, :, side - rim :].add(from_right)
    return interior


def segment_kernel(segs, terms, rim, foot_ref, off_ref, band_ref, w_ref, win_ref, obs_ref, rows_ref,
                   rows_t_ref, cols_ref, cols_t_ref, canvas_ref, rims_ref, acc_ref, res_ref):
    f32 = jnp.float32
    bf = jnp.bfloat16
    pix = obs_ref.shape[1]
    width = canvas_ref.shape[2]
    tall = pix + 8
    tile = 128
    row_anchor = lax.axis_index("sky") * pix - rim
    col_anchor = lax.axis_index("visit") * pix - rim
    canvas_ref[...] = jnp.zeros(canvas_ref.shape, f32)

    def one_segment(s, carry):
        band = band_ref[s]
        top = foot_ref[s, 0] * tile + off_ref[s, 0] - row_anchor
        left_at = foot_ref[s, 1] * tile + off_ref[s, 1] - col_anchor
        base8 = lax.shift_left(lax.shift_right_logical(top, 3), 3)
        def blurred(k):
            left = jnp.dot(rows_ref[k], win_ref[s], preferred_element_type=f32).astype(bf)
            return w_ref[s, k] * jnp.dot(left, cols_t_ref[k], preferred_element_type=f32)

        def forward(k, c):
            acc_ref[...] += blurred(k)
            return c

        acc_ref[...] = blurred(0)
        lax.fori_loop(1, terms, forward, 0)
        res_ref[...] = (acc_ref[...] - obs_ref[s].astype(f32)).astype(bf)
        def spread(k):
            right = jnp.dot(res_ref[...], cols_ref[k], preferred_element_type=f32).astype(bf)
            return w_ref[s, k] * jnp.dot(rows_t_ref[k], right, preferred_element_type=f32)

        def backward(k, c):
            acc_ref[...] += spread(k)
            return c

        acc_ref[...] = spread(0)
        lax.fori_loop(1, terms, backward, 0)
        adj = acc_ref[...].astype(bf)
        src_col = lax.broadcasted_iota(jnp.int32, (pix, width), 0)
        dst_col = lax.broadcasted_iota(jnp.int32, (pix, width), 1)
        col_shift = (dst_col == src_col + left_at).astype(bf)
        spread_cols = jnp.dot(adj, col_shift, preferred_element_type=f32).astype(bf)
        dst_row = lax.broadcasted_iota(jnp.int32, (tall, pix), 0)
        src_row = lax.broadcasted_iota(jnp.int32, (tall, pix), 1)
        row_shift = (dst_row == src_row + (top - base8)).astype(bf)
        placed = jnp.dot(row_shift, spread_cols, preferred_element_type=f32)
        rows_at = pl.ds(pl.multiple_of(base8, 8), tall)
        canvas_ref[band, rows_at, :] += placed
        return carry

    lax.fori_loop(0, segs, one_segment, 0)
    half = rims_ref.shape[2] // 2
    rows = rims_ref.shape[1]
    rims_ref[:, :, :half] = canvas_ref[:, :rows, :half].astype(rims_ref.dtype)
    rims_ref[:, :, half:] = canvas_ref[:, :rows, width - half :].astype(rims_ref.dtype)


def accumulate(windows, observed, footprint, offsets, segment_band, psf_rows, psf_cols,
               psf_weights, rim, extended_shape):
    segs, pix, _ = observed.shape
    terms = psf_rows.shape[0]
    bands, full, _ = extended_shape
    rows_t = jnp.swapaxes(psf_rows, 1, 2)
    cols_t = jnp.swapaxes(psf_cols, 1, 2)
    smem = pl.BlockSpec(memory_space=pltpu.SMEM)
    vmem = pl.BlockSpec(memory_space=pltpu.VMEM)
    flops = segs * (terms * 4 * 2 * pix ** 3 + 6 * pix * pix * full)
    moved = 2 * pix * pix * (3 * segs + 4 * terms) + 4 * bands * (full + 8) * full
    return pl.pallas_call(
        functools.partial(segment_kernel, segs, terms, rim),
        in_specs=[smem, smem, smem, smem, vmem, vmem, vmem, vmem, vmem, vmem],
        out_specs=(vmem, vmem),
        out_shape=(
            jax.ShapeDtypeStruct((bands, full + 8, full), jnp.float32),
            jax.ShapeDtypeStruct((bands, full, 2 * rim), jnp.bfloat16),
        ),
        scratch_shapes=[
            pltpu.VMEM((pix, pix), jnp.float32),
            pltpu.VMEM((pix, pix), jnp.bfloat16),
        ],
        compiler_params=pltpu.CompilerParams(vmem_limit_bytes=62 * 1024 * 1024),
        cost_estimate=pl.CostEstimate(flops=flops, bytes_accessed=moved, transcendentals=0),
    )(footprint, offsets, segment_band, psf_weights, windows, observed, psf_rows, rows_t,
      psf_cols, cols_t)


def per_device(
    sky_image,
    observed,
    footprint,
    segment_band,
    offsets,
    psf_rows,
    psf_cols,
    psf_weights,
    step_sizes,
):
    pixels = observed.shape[1]
    rim = (pixels // TILE + 1) // 2 * TILE
    block_side = sky_image.shape[1]
    segs = observed.shape[0]
    sky_bf = sky_image.astype(jnp.bfloat16)
    row_anchor = lax.axis_index("sky") * block_side - rim
    col_anchor = lax.axis_index("visit") * block_side - rim
    top_rows = footprint[:, 0] * TILE + offsets[:, 0] - row_anchor
    left_cols = footprint[:, 1] * TILE + offsets[:, 1] - col_anchor
    at = [(segment_band[s], top_rows[s], left_cols[s]) for s in range(segs)]
    at, sky_bf = lax.optimization_barrier((at, sky_bf))
    extended = halo(sky_bf, rim)
    windows = jnp.stack(
        [
            lax.dynamic_slice(
                extended, at[s], (1, pixels, pixels), allow_negative_indices=False
            )[0]
            for s in range(segs)
        ]
    )
    canvas, rims = accumulate(
        windows, observed, footprint, offsets, segment_band, psf_rows, psf_cols, psf_weights, rim,
        extended.shape,
    )
    gradient = fold(canvas, rims, rim, extended.shape[2])
    return sky_image - step_sizes[:, None, None] * gradient


def solution(mesh):
    placed = (
        P(None, "sky", "visit"),
        P(("sky", "visit"), None, None),
        P(("sky", "visit"), None),
        P(("sky", "visit")),
        P(("sky", "visit"), None),
        P(),
        P(),
        P(("sky", "visit"), None),
        P(),
    )
    return jax.shard_map(
        per_device, mesh=mesh, in_specs=placed, out_specs=P(None, "sky", "visit"), check_vma=False
    )
```

```python
import functools

import jax
import jax.numpy as jnp
from jax import lax
from jax.experimental import pallas as pl
from jax.experimental.pallas import tpu as pltpu
from jax.sharding import PartitionSpec as P

TILE = 128


def shift(value, axis, by):
    count = lax.axis_size(axis)
    pairs = [(i, i + by) for i in range(count) if 0 <= i + by < count]
    return lax.ppermute(value, axis, pairs)


def halo(block, rim):
    side = block.shape[1]
    up = shift(block[:, side - rim :, :], "sky", 1)
    down = shift(block[:, :rim, :], "sky", -1)
    left = shift(block[:, :, side - rim :], "visit", 1)
    right = shift(block[:, :, :rim], "visit", -1)
    to_right = jnp.concatenate([up[:, :, side - rim :], down[:, :, side - rim :]], axis=1)
    to_left = jnp.concatenate([up[:, :, :rim], down[:, :, :rim]], axis=1)
    to_right, to_left, left, right = lax.optimization_barrier((to_right, to_left, left, right))
    from_left = shift(to_right, "visit", 1)
    from_right = shift(to_left, "visit", -1)
    top = jnp.concatenate([from_left[:, :rim], up, from_right[:, :rim]], axis=2)
    middle = jnp.concatenate([left, block, right], axis=2)
    bottom = jnp.concatenate([from_left[:, rim:], down, from_right[:, rim:]], axis=2)
    return jnp.concatenate([top, middle, bottom], axis=1)


def fold(canvas, rims, rim, full):
    side = full - 2 * rim
    bf = jnp.bfloat16
    lo, hi = slice(0, rim), slice(full - rim, full)
    mid = slice(rim, rim + side)
    first, second = slice(0, rim), slice(rim, 2 * rim)
    to_left = jnp.concatenate([rims[:, lo, first], rims[:, hi, first]], axis=1)
    to_right = jnp.concatenate([rims[:, lo, second], rims[:, hi, second]], axis=1)
    got_right = shift(to_left, "visit", -1).astype(jnp.float32)
    got_left = shift(to_right, "visit", 1).astype(jnp.float32)
    top = canvas[:, lo, :]
    bottom = canvas[:, hi, :]
    top = top + jnp.concatenate([got_left[:, :rim], got_right[:, :rim]], axis=2)
    bottom = bottom + jnp.concatenate([got_left[:, rim:], got_right[:, rim:]], axis=2)
    from_down = shift(top.astype(bf), "sky", -1).astype(jnp.float32)
    from_up = shift(bottom.astype(bf), "sky", 1).astype(jnp.float32)
    from_right = shift(rims[:, mid, first], "visit", -1).astype(jnp.float32)
    from_left = shift(rims[:, mid, second], "visit", 1).astype(jnp.float32)
    interior = canvas[:, mid, :]
    interior = interior.at[:, :rim, :].add(from_up)
    interior = interior.at[:, side - rim :, :].add(from_down)
    interior = interior.at[:, :, :rim].add(from_left)
    interior = interior.at[:, :, side - rim :].add(from_right)
    return interior


def segment_kernel(segs, terms, rim, foot_ref, off_ref, band_ref, w_ref, win_ref, obs_ref, rows_ref,
                   rows_t_ref, cols_ref, cols_t_ref, canvas_ref, rims_ref, acc_ref, res_ref, sides_ref):
    f32 = jnp.float32
    bf = jnp.bfloat16
    pix = obs_ref.shape[1]
    width = canvas_ref.shape[2] + sides_ref.shape[2]
    half = sides_ref.shape[2] // 2
    tall = pix + 8
    tile = 128
    row_anchor = lax.axis_index("sky") * pix - rim
    col_anchor = lax.axis_index("visit") * pix - rim
    canvas_ref[...] = jnp.zeros(canvas_ref.shape, f32)
    sides_ref[...] = jnp.zeros(sides_ref.shape, f32)

    def one_segment(s, carry):
        band = band_ref[s]
        top = foot_ref[s, 0] * tile + off_ref[s, 0] - row_anchor
        left_at = foot_ref[s, 1] * tile + off_ref[s, 1] - col_anchor
        base8 = lax.shift_left(lax.shift_right_logical(top, 3), 3)
        def blurred(k):
            left = jnp.dot(rows_ref[k], win_ref[s], preferred_element_type=f32).astype(bf)
            return w_ref[s, k] * jnp.dot(left, cols_t_ref[k], preferred_element_type=f32)

        def forward(k, c):
            acc_ref[...] += blurred(k)
            return c

        acc_ref[...] = blurred(0)
        lax.fori_loop(1, terms, forward, 0)
        res_ref[...] = (acc_ref[...] - obs_ref[s].astype(f32)).astype(bf)
        def spread(k):
            right = jnp.dot(res_ref[...], cols_ref[k], preferred_element_type=f32).astype(bf)
            return w_ref[s, k] * jnp.dot(rows_t_ref[k], right, preferred_element_type=f32)

        def backward(k, c):
            acc_ref[...] += spread(k)
            return c

        acc_ref[...] = spread(0)
        lax.fori_loop(1, terms, backward, 0)
        adj = acc_ref[...].astype(bf)
        src_col = lax.broadcasted_iota(jnp.int32, (pix, width), 0)
        dst_col = lax.broadcasted_iota(jnp.int32, (pix, width), 1)
        col_shift = (dst_col == src_col + left_at).astype(bf)
        spread_cols = jnp.dot(adj, col_shift, preferred_element_type=f32).astype(bf)
        dst_row = lax.broadcasted_iota(jnp.int32, (tall, pix), 0)
        src_row = lax.broadcasted_iota(jnp.int32, (tall, pix), 1)
        row_shift = (dst_row == src_row + (top - base8)).astype(bf)
        placed = jnp.dot(row_shift, spread_cols, preferred_element_type=f32)
        rows_at = pl.ds(pl.multiple_of(base8, 8), tall)
        canvas_ref[band, rows_at, :] += placed[:, half : width - half]
        sides_ref[band, rows_at, :half] += placed[:, :half]
        sides_ref[band, rows_at, half:] += placed[:, width - half :]
        return carry

    lax.fori_loop(0, segs, one_segment, 0)
    rows = rims_ref.shape[1]
    rims_ref[...] = sides_ref[:, :rows, :].astype(rims_ref.dtype)


def accumulate(windows, observed, footprint, offsets, segment_band, psf_rows, psf_cols,
               psf_weights, rim, extended_shape):
    segs, pix, _ = observed.shape
    terms = psf_rows.shape[0]
    bands, full, _ = extended_shape
    rows_t = jnp.swapaxes(psf_rows, 1, 2)
    cols_t = jnp.swapaxes(psf_cols, 1, 2)
    smem = pl.BlockSpec(memory_space=pltpu.SMEM)
    vmem = pl.BlockSpec(memory_space=pltpu.VMEM)
    flops = segs * (terms * 4 * 2 * pix ** 3 + 6 * pix * pix * full)
    moved = 2 * pix * pix * (3 * segs + 4 * terms) + 4 * bands * (full + 8) * full
    return pl.pallas_call(
        functools.partial(segment_kernel, segs, terms, rim),
        in_specs=[smem, smem, smem, smem, vmem, vmem, vmem, vmem, vmem, vmem],
        out_specs=(vmem, vmem),
        out_shape=(
            jax.ShapeDtypeStruct((bands, full + 8, full - 2 * rim), jnp.float32),
            jax.ShapeDtypeStruct((bands, full, 2 * rim), jnp.bfloat16),
        ),
        scratch_shapes=[
            pltpu.VMEM((pix, pix), jnp.float32),
            pltpu.VMEM((pix, pix), jnp.bfloat16),
            pltpu.VMEM((bands, full + 8, 2 * rim), jnp.float32),
        ],
        compiler_params=pltpu.CompilerParams(vmem_limit_bytes=62 * 1024 * 1024),
        cost_estimate=pl.CostEstimate(flops=flops, bytes_accessed=moved, transcendentals=0),
    )(footprint, offsets, segment_band, psf_weights, windows, observed, psf_rows, rows_t,
      psf_cols, cols_t)


def per_device(
    sky_image,
    observed,
    footprint,
    segment_band,
    offsets,
    psf_rows,
    psf_cols,
    psf_weights,
    step_sizes,
):
    pixels = observed.shape[1]
    rim = (pixels // TILE + 1) // 2 * TILE
    block_side = sky_image.shape[1]
    segs = observed.shape[0]
    sky_bf = sky_image.astype(jnp.bfloat16)
    row_anchor = lax.axis_index("sky") * block_side - rim
    col_anchor = lax.axis_index("visit") * block_side - rim
    top_rows = footprint[:, 0] * TILE + offsets[:, 0] - row_anchor
    left_cols = footprint[:, 1] * TILE + offsets[:, 1] - col_anchor
    at = [(segment_band[s], top_rows[s], left_cols[s]) for s in range(segs)]
    at, sky_bf = lax.optimization_barrier((at, sky_bf))
    extended = halo(sky_bf, rim)
    windows = jnp.stack(
        [
            lax.dynamic_slice(
                extended, at[s], (1, pixels, pixels), allow_negative_indices=False
            )[0]
            for s in range(segs)
        ]
    )
    canvas, rims = accumulate(
        windows, observed, footprint, offsets, segment_band, psf_rows, psf_cols, psf_weights, rim,
        extended.shape,
    )
    gradient = fold(canvas, rims, rim, extended.shape[2])
    return sky_image - step_sizes[:, None, None] * gradient


def solution(mesh):
    placed = (
        P(None, "sky", "visit"),
        P(("sky", "visit"), None, None),
        P(("sky", "visit"), None),
        P(("sky", "visit")),
        P(("sky", "visit"), None),
        P(),
        P(),
        P(("sky", "visit"), None),
        P(),
    )
    return jax.shard_map(
        per_device, mesh=mesh, in_specs=placed, out_specs=P(None, "sky", "visit"), check_vma=False
    )
```

```python
import functools

import jax
import jax.numpy as jnp
from jax import lax
from jax.experimental import pallas as pl
from jax.experimental.pallas import tpu as pltpu
from jax.sharding import PartitionSpec as P

TILE = 128


def shift(value, axis, by):
    count = lax.axis_size(axis)
    pairs = [(i, i + by) for i in range(count) if 0 <= i + by < count]
    return lax.ppermute(value, axis, pairs)


def halo(block, rim):
    side = block.shape[1]
    up = shift(block[:, side - rim :, :], "sky", 1)
    down = shift(block[:, :rim, :], "sky", -1)
    left = shift(block[:, :, side - rim :], "visit", 1)
    right = shift(block[:, :, :rim], "visit", -1)
    to_right = jnp.concatenate([up[:, :, side - rim :], down[:, :, side - rim :]], axis=1)
    to_left = jnp.concatenate([up[:, :, :rim], down[:, :, :rim]], axis=1)
    to_right, to_left, left, right = lax.optimization_barrier((to_right, to_left, left, right))
    from_left = shift(to_right, "visit", 1)
    from_right = shift(to_left, "visit", -1)
    top = jnp.concatenate([from_left[:, :rim], up, from_right[:, :rim]], axis=2)
    middle = jnp.concatenate([left, block, right], axis=2)
    bottom = jnp.concatenate([from_left[:, rim:], down, from_right[:, rim:]], axis=2)
    return jnp.concatenate([top, middle, bottom], axis=1)


def fold(canvas, pieces, rim, full):
    side = full - 2 * rim
    bf = jnp.bfloat16
    lo, hi = slice(0, rim), slice(full - rim, full)
    mid = slice(rim, rim + side)
    to_left, to_right, mid_left, mid_right = pieces
    got_right = shift(to_left, "visit", -1).astype(jnp.float32)
    got_left = shift(to_right, "visit", 1).astype(jnp.float32)
    top = canvas[:, lo, :]
    bottom = canvas[:, hi, :]
    top = top + jnp.concatenate([got_left[:, :rim], got_right[:, :rim]], axis=2)
    bottom = bottom + jnp.concatenate([got_left[:, rim:], got_right[:, rim:]], axis=2)
    from_down = shift(top.astype(bf), "sky", -1).astype(jnp.float32)
    from_up = shift(bottom.astype(bf), "sky", 1).astype(jnp.float32)
    from_right = shift(mid_left, "visit", -1).astype(jnp.float32)
    from_left = shift(mid_right, "visit", 1).astype(jnp.float32)
    interior = canvas[:, mid, :]
    interior = interior.at[:, :rim, :].add(from_up)
    interior = interior.at[:, side - rim :, :].add(from_down)
    interior = interior.at[:, :, :rim].add(from_left)
    interior = interior.at[:, :, side - rim :].add(from_right)
    return interior


def segment_kernel(segs, terms, rim, foot_ref, off_ref, band_ref, w_ref, win_ref, obs_ref, rows_ref,
                   rows_t_ref, cols_ref, cols_t_ref, canvas_ref, to_left_ref, to_right_ref, mid_left_ref,
                   mid_right_ref, acc_ref, res_ref, sides_ref):
    f32 = jnp.float32
    bf = jnp.bfloat16
    pix = obs_ref.shape[1]
    width = canvas_ref.shape[2] + sides_ref.shape[2]
    half = sides_ref.shape[2] // 2
    tall = pix + 8
    tile = 128
    row_anchor = lax.axis_index("sky") * pix - rim
    col_anchor = lax.axis_index("visit") * pix - rim
    canvas_ref[...] = jnp.zeros(canvas_ref.shape, f32)
    sides_ref[...] = jnp.zeros(sides_ref.shape, f32)

    def one_segment(s, carry):
        band = band_ref[s]
        top = foot_ref[s, 0] * tile + off_ref[s, 0] - row_anchor
        left_at = foot_ref[s, 1] * tile + off_ref[s, 1] - col_anchor
        base8 = lax.shift_left(lax.shift_right_logical(top, 3), 3)
        def blurred(k):
            left = jnp.dot(rows_ref[k], win_ref[s], preferred_element_type=f32).astype(bf)
            return w_ref[s, k] * jnp.dot(left, cols_t_ref[k], preferred_element_type=f32)

        def forward(k, c):
            acc_ref[...] += blurred(k)
            return c

        acc_ref[...] = blurred(0)
        lax.fori_loop(1, terms, forward, 0)
        res_ref[...] = (acc_ref[...] - obs_ref[s].astype(f32)).astype(bf)
        def spread(k):
            right = jnp.dot(res_ref[...], cols_ref[k], preferred_element_type=f32).astype(bf)
            return w_ref[s, k] * jnp.dot(rows_t_ref[k], right, preferred_element_type=f32)

        def backward(k, c):
            acc_ref[...] += spread(k)
            return c

        acc_ref[...] = spread(0)
        lax.fori_loop(1, terms, backward, 0)
        adj = acc_ref[...].astype(bf)
        src_col = lax.broadcasted_iota(jnp.int32, (pix, width), 0)
        dst_col = lax.broadcasted_iota(jnp.int32, (pix, width), 1)
        col_shift = (dst_col == src_col + left_at).astype(bf)
        spread_cols = jnp.dot(adj, col_shift, preferred_element_type=f32).astype(bf)
        dst_row = lax.broadcasted_iota(jnp.int32, (tall, pix), 0)
        src_row = lax.broadcasted_iota(jnp.int32, (tall, pix), 1)
        row_shift = (dst_row == src_row + (top - base8)).astype(bf)
        placed = jnp.dot(row_shift, spread_cols, preferred_element_type=f32)
        rows_at = pl.ds(pl.multiple_of(base8, 8), tall)
        canvas_ref[band, rows_at, :] += placed[:, half : width - half]
        sides_ref[band, rows_at, :half] += placed[:, :half]
        sides_ref[band, rows_at, half:] += placed[:, width - half :]
        return carry

    lax.fori_loop(0, segs, one_segment, 0)
    low, high = slice(0, half), slice(half, 2 * half)
    far = width - half
    to_left_ref[:, :half, :] = sides_ref[:, :half, low].astype(bf)
    to_left_ref[:, half:, :] = sides_ref[:, far:width, low].astype(bf)
    to_right_ref[:, :half, :] = sides_ref[:, :half, high].astype(bf)
    to_right_ref[:, half:, :] = sides_ref[:, far:width, high].astype(bf)
    mid_left_ref[...] = sides_ref[:, half:far, low].astype(bf)
    mid_right_ref[...] = sides_ref[:, half:far, high].astype(bf)


def accumulate(windows, observed, footprint, offsets, segment_band, psf_rows, psf_cols,
               psf_weights, rim, extended_shape):
    segs, pix, _ = observed.shape
    terms = psf_rows.shape[0]
    bands, full, _ = extended_shape
    rows_t = jnp.swapaxes(psf_rows, 1, 2)
    cols_t = jnp.swapaxes(psf_cols, 1, 2)
    smem = pl.BlockSpec(memory_space=pltpu.SMEM)
    vmem = pl.BlockSpec(memory_space=pltpu.VMEM)
    flops = segs * (terms * 4 * 2 * pix ** 3 + 6 * pix * pix * full)
    moved = 2 * pix * pix * (3 * segs + 4 * terms) + 4 * bands * (full + 8) * full
    return pl.pallas_call(
        functools.partial(segment_kernel, segs, terms, rim),
        in_specs=[smem, smem, smem, smem, vmem, vmem, vmem, vmem, vmem, vmem],
        out_specs=(vmem, vmem, vmem, vmem, vmem),
        out_shape=(
            jax.ShapeDtypeStruct((bands, full + 8, full - 2 * rim), jnp.float32),
        )
        + (jax.ShapeDtypeStruct((bands, full - 2 * rim, rim), jnp.bfloat16),) * 4,
        scratch_shapes=[
            pltpu.VMEM((pix, pix), jnp.float32),
            pltpu.VMEM((pix, pix), jnp.bfloat16),
            pltpu.VMEM((bands, full + 8, 2 * rim), jnp.float32),
        ],
        compiler_params=pltpu.CompilerParams(vmem_limit_bytes=62 * 1024 * 1024),
        cost_estimate=pl.CostEstimate(flops=flops, bytes_accessed=moved, transcendentals=0),
    )(footprint, offsets, segment_band, psf_weights, windows, observed, psf_rows, rows_t,
      psf_cols, cols_t)


def per_device(
    sky_image,
    observed,
    footprint,
    segment_band,
    offsets,
    psf_rows,
    psf_cols,
    psf_weights,
    step_sizes,
):
    pixels = observed.shape[1]
    rim = (pixels // TILE + 1) // 2 * TILE
    block_side = sky_image.shape[1]
    segs = observed.shape[0]
    sky_bf = sky_image.astype(jnp.bfloat16)
    row_anchor = lax.axis_index("sky") * block_side - rim
    col_anchor = lax.axis_index("visit") * block_side - rim
    top_rows = footprint[:, 0] * TILE + offsets[:, 0] - row_anchor
    left_cols = footprint[:, 1] * TILE + offsets[:, 1] - col_anchor
    at = [(segment_band[s], top_rows[s], left_cols[s]) for s in range(segs)]
    at, sky_bf = lax.optimization_barrier((at, sky_bf))
    extended = halo(sky_bf, rim)
    windows = jnp.stack(
        [
            lax.dynamic_slice(
                extended, at[s], (1, pixels, pixels), allow_negative_indices=False
            )[0]
            for s in range(segs)
        ]
    )
    canvas, *pieces = accumulate(
        windows, observed, footprint, offsets, segment_band, psf_rows, psf_cols, psf_weights, rim,
        extended.shape,
    )
    gradient = fold(canvas, pieces, rim, extended.shape[2])
    return sky_image - step_sizes[:, None, None] * gradient


def solution(mesh):
    placed = (
        P(None, "sky", "visit"),
        P(("sky", "visit"), None, None),
        P(("sky", "visit"), None),
        P(("sky", "visit")),
        P(("sky", "visit"), None),
        P(),
        P(),
        P(("sky", "visit"), None),
        P(),
    )
    return jax.shard_map(
        per_device, mesh=mesh, in_specs=placed, out_specs=P(None, "sky", "visit"), check_vma=False
    )
```

```python
import functools

import jax
import jax.numpy as jnp
from jax import lax
from jax.experimental import pallas as pl
from jax.experimental.pallas import tpu as pltpu
from jax.sharding import PartitionSpec as P

TILE = 128


def shift(value, axis, by):
    count = lax.axis_size(axis)
    pairs = [(i, i + by) for i in range(count) if 0 <= i + by < count]
    return lax.ppermute(value, axis, pairs)


def halo(block, rim):
    side = block.shape[1]
    up = shift(block[:, side - rim :, :], "sky", 1)
    down = shift(block[:, :rim, :], "sky", -1)
    left = shift(block[:, :, side - rim :], "visit", 1)
    right = shift(block[:, :, :rim], "visit", -1)
    to_right = jnp.concatenate([up[:, :, side - rim :], down[:, :, side - rim :]], axis=1)
    to_left = jnp.concatenate([up[:, :, :rim], down[:, :, :rim]], axis=1)
    to_right, to_left, left, right = lax.optimization_barrier((to_right, to_left, left, right))
    from_left = shift(to_right, "visit", 1)
    from_right = shift(to_left, "visit", -1)
    top = jnp.concatenate([from_left[:, :rim], up, from_right[:, :rim]], axis=2)
    middle = jnp.concatenate([left, block, right], axis=2)
    bottom = jnp.concatenate([from_left[:, rim:], down, from_right[:, rim:]], axis=2)
    return jnp.concatenate([top, middle, bottom], axis=1)


def fold(canvas, pieces, rim, full):
    side = full - 2 * rim
    bf = jnp.bfloat16
    lo, hi = slice(0, rim), slice(full - rim, full)
    mid = slice(rim, rim + side)
    to_left, to_right, mid_left, mid_right = pieces
    got_right = shift(to_left, "visit", -1).astype(jnp.float32)
    got_left = shift(to_right, "visit", 1).astype(jnp.float32)
    top = canvas[:, lo, :]
    bottom = canvas[:, hi, :]
    top = top + jnp.concatenate([got_left[:, :rim], got_right[:, :rim]], axis=2)
    bottom = bottom + jnp.concatenate([got_left[:, rim:], got_right[:, rim:]], axis=2)
    from_down = shift(top.astype(bf), "sky", -1).astype(jnp.float32)
    from_up = shift(bottom.astype(bf), "sky", 1).astype(jnp.float32)
    from_right = shift(mid_left, "visit", -1).astype(jnp.float32)
    from_left = shift(mid_right, "visit", 1).astype(jnp.float32)
    rest = side - rim
    interior = canvas[:, mid, :]
    interior = interior + jnp.pad(from_up, ((0, 0), (0, rest), (0, 0)))
    interior = interior + jnp.pad(from_down, ((0, 0), (rest, 0), (0, 0)))
    interior = interior + jnp.pad(from_left, ((0, 0), (0, 0), (0, rest)))
    interior = interior + jnp.pad(from_right, ((0, 0), (0, 0), (rest, 0)))
    return interior


def segment_kernel(segs, terms, rim, foot_ref, off_ref, band_ref, w_ref, win_ref, obs_ref, rows_ref,
                   rows_t_ref, cols_ref, cols_t_ref, canvas_ref, to_left_ref, to_right_ref, mid_left_ref,
                   mid_right_ref, acc_ref, res_ref, sides_ref):
    f32 = jnp.float32
    bf = jnp.bfloat16
    pix = obs_ref.shape[1]
    width = canvas_ref.shape[2] + sides_ref.shape[2]
    half = sides_ref.shape[2] // 2
    tall = pix + 8
    tile = 128
    row_anchor = lax.axis_index("sky") * pix - rim
    col_anchor = lax.axis_index("visit") * pix - rim
    canvas_ref[...] = jnp.zeros(canvas_ref.shape, f32)
    sides_ref[...] = jnp.zeros(sides_ref.shape, f32)

    def one_segment(s, carry):
        band = band_ref[s]
        top = foot_ref[s, 0] * tile + off_ref[s, 0] - row_anchor
        left_at = foot_ref[s, 1] * tile + off_ref[s, 1] - col_anchor
        base8 = lax.shift_left(lax.shift_right_logical(top, 3), 3)
        def blurred(k):
            left = jnp.dot(rows_ref[k], win_ref[s], preferred_element_type=f32).astype(bf)
            return w_ref[s, k] * jnp.dot(left, cols_t_ref[k], preferred_element_type=f32)

        def forward(k, c):
            acc_ref[...] += blurred(k)
            return c

        acc_ref[...] = blurred(0)
        lax.fori_loop(1, terms, forward, 0)
        res_ref[...] = (acc_ref[...] - obs_ref[s].astype(f32)).astype(bf)
        def spread(k):
            right = jnp.dot(res_ref[...], cols_ref[k], preferred_element_type=f32).astype(bf)
            return w_ref[s, k] * jnp.dot(rows_t_ref[k], right, preferred_element_type=f32)

        def backward(k, c):
            acc_ref[...] += spread(k)
            return c

        acc_ref[...] = spread(0)
        lax.fori_loop(1, terms, backward, 0)
        adj = acc_ref[...].astype(bf)
        src_col = lax.broadcasted_iota(jnp.int32, (pix, width), 0)
        dst_col = lax.broadcasted_iota(jnp.int32, (pix, width), 1)
        col_shift = (dst_col == src_col + left_at).astype(bf)
        spread_cols = jnp.dot(adj, col_shift, preferred_element_type=f32).astype(bf)
        dst_row = lax.broadcasted_iota(jnp.int32, (tall, pix), 0)
        src_row = lax.broadcasted_iota(jnp.int32, (tall, pix), 1)
        row_shift = (dst_row == src_row + (top - base8)).astype(bf)
        placed = jnp.dot(row_shift, spread_cols, preferred_element_type=f32)
        rows_at = pl.ds(pl.multiple_of(base8, 8), tall)
        canvas_ref[band, rows_at, :] += placed[:, half : width - half]
        sides_ref[band, rows_at, :half] += placed[:, :half]
        sides_ref[band, rows_at, half:] += placed[:, width - half :]
        return carry

    lax.fori_loop(0, segs, one_segment, 0)
    low, high = slice(0, half), slice(half, 2 * half)
    far = width - half
    to_left_ref[:, :half, :] = sides_ref[:, :half, low].astype(bf)
    to_left_ref[:, half:, :] = sides_ref[:, far:width, low].astype(bf)
    to_right_ref[:, :half, :] = sides_ref[:, :half, high].astype(bf)
    to_right_ref[:, half:, :] = sides_ref[:, far:width, high].astype(bf)
    mid_left_ref[...] = sides_ref[:, half:far, low].astype(bf)
    mid_right_ref[...] = sides_ref[:, half:far, high].astype(bf)


def accumulate(windows, observed, footprint, offsets, segment_band, psf_rows, psf_cols,
               psf_weights, rim, extended_shape):
    segs, pix, _ = observed.shape
    terms = psf_rows.shape[0]
    bands, full, _ = extended_shape
    rows_t = jnp.swapaxes(psf_rows, 1, 2)
    cols_t = jnp.swapaxes(psf_cols, 1, 2)
    smem = pl.BlockSpec(memory_space=pltpu.SMEM)
    vmem = pl.BlockSpec(memory_space=pltpu.VMEM)
    flops = segs * (terms * 4 * 2 * pix ** 3 + 6 * pix * pix * full)
    moved = 2 * pix * pix * (3 * segs + 4 * terms) + 4 * bands * (full + 8) * full
    return pl.pallas_call(
        functools.partial(segment_kernel, segs, terms, rim),
        in_specs=[smem, smem, smem, smem, vmem, vmem, vmem, vmem, vmem, vmem],
        out_specs=(vmem, vmem, vmem, vmem, vmem),
        out_shape=(
            jax.ShapeDtypeStruct((bands, full + 8, full - 2 * rim), jnp.float32),
        )
        + (jax.ShapeDtypeStruct((bands, full - 2 * rim, rim), jnp.bfloat16),) * 4,
        scratch_shapes=[
            pltpu.VMEM((pix, pix), jnp.float32),
            pltpu.VMEM((pix, pix), jnp.bfloat16),
            pltpu.VMEM((bands, full + 8, 2 * rim), jnp.float32),
        ],
        compiler_params=pltpu.CompilerParams(vmem_limit_bytes=62 * 1024 * 1024),
        cost_estimate=pl.CostEstimate(flops=flops, bytes_accessed=moved, transcendentals=0),
    )(footprint, offsets, segment_band, psf_weights, windows, observed, psf_rows, rows_t,
      psf_cols, cols_t)


def per_device(
    sky_image,
    observed,
    footprint,
    segment_band,
    offsets,
    psf_rows,
    psf_cols,
    psf_weights,
    step_sizes,
):
    pixels = observed.shape[1]
    rim = (pixels // TILE + 1) // 2 * TILE
    block_side = sky_image.shape[1]
    segs = observed.shape[0]
    sky_bf = sky_image.astype(jnp.bfloat16)
    row_anchor = lax.axis_index("sky") * block_side - rim
    col_anchor = lax.axis_index("visit") * block_side - rim
    top_rows = footprint[:, 0] * TILE + offsets[:, 0] - row_anchor
    left_cols = footprint[:, 1] * TILE + offsets[:, 1] - col_anchor
    at = [(segment_band[s], top_rows[s], left_cols[s]) for s in range(segs)]
    at, sky_bf = lax.optimization_barrier((at, sky_bf))
    extended = halo(sky_bf, rim)
    windows = jnp.stack(
        [
            lax.dynamic_slice(
                extended, at[s], (1, pixels, pixels), allow_negative_indices=False
            )[0]
            for s in range(segs)
        ]
    )
    canvas, *pieces = accumulate(
        windows, observed, footprint, offsets, segment_band, psf_rows, psf_cols, psf_weights, rim,
        extended.shape,
    )
    gradient = fold(canvas, pieces, rim, extended.shape[2])
    return sky_image - step_sizes[:, None, None] * gradient


def solution(mesh):
    placed = (
        P(None, "sky", "visit"),
        P(("sky", "visit"), None, None),
        P(("sky", "visit"), None),
        P(("sky", "visit")),
        P(("sky", "visit"), None),
        P(),
        P(),
        P(("sky", "visit"), None),
        P(),
    )
    return jax.shard_map(
        per_device, mesh=mesh, in_specs=placed, out_specs=P(None, "sky", "visit"), check_vma=False
    )
```
